32 devices in a mesh: groups: 2 (over x), wide: 8 (over z, y), narrow: 2 (over core).
Axes of the slice: x: 2, y: 2, z: 4, core: 2. Of those that a mesh axis runs over, the one named last changes fastest.
Arguments:
- queries: bfloat16 [8192, 1024], P(('groups', 'narrow', 'wide')), parts along dimension 0, may hold values from -8 to 8
- keys: bfloat16 [8192, 1024], P(('groups', 'narrow', 'wide')), parts along dimension 0, may hold values from -8 to 8
- values: bfloat16 [8192, 1024], P(('groups', 'narrow', 'wide')), parts along dimension 0, may hold values from -6 to 6
- block_lists: int32 [16, 32, 16], P(('groups', 'wide'), 'narrow'), parts along dimension 0, may hold values from 0 to 31, as said below
- block_counts: int32 [16, 32], P(('groups', 'wide'), 'narrow'), parts along dimension 0, may hold values from 1 to 16
Outputs:
- attention: bfloat16 [8192, 1024], P(('groups', 'narrow', 'wide')), parts along dimension 0
The draws below stay inside these ranges and needn't reach their ends.
There are 2 independent parts, one for each index of `groups`. The reference program is written for one: setup_inputs(seed, part) draws one part's arguments, and reference() takes and returns one part's arrays. A program takes and returns all parts, laid end to end along the dimension named above; each array names one. Nothing has to cross between parts.
Inputs may be any that keep to these rules, and one draw needn't show every extreme that they name: `block_lists`: entries are block indices; the first entry of each list is the query block's own index and the first block_counts entries of a list are distinct; later entries are ignored.
All inputs are finite; a program needn't handle non-finite values.
Results may differ from the reference program's by a relative error of at most 0.0044.
Values may be sent and summed in bfloat16 or wider, within the bound.
No kernel may reach another device: no remote copies, remote signals or barrier semaphores. Data moves between devices by JAX's collectives and lax.ppermute only.
A program may use at most 128 MiB of HBM per device.

```python
import math
import jax
import jax.numpy as jnp
from jax import lax

HEAD_FEATURES = 128
BLOCK = 128
HEADS = 8
TOKENS = 4096
NQB = 32
MAXB = 16


def drawn_rows(key, salt):
    base = jax.random.fold_in(key, salt)
    return jnp.clip(jax.random.normal(base, (TOKENS, HEADS * HEAD_FEATURES), jnp.float32), -4.0, 4.0)


def draw_queries(key, part):
    row_vals = drawn_rows(key, 1)
    return row_vals.astype(jnp.bfloat16)


def draw_keys(key, part):
    row_vals = drawn_rows(key, 3)
    return row_vals.astype(jnp.bfloat16)


def draw_block_lists(key, part):
    logit_scores = jax.random.randint(jax.random.fold_in(key, 27), (HEADS, NQB, NQB - 1), 0, 1 << 20) * NQB
    logit_scores = logit_scores + jnp.arange(NQB - 1, dtype=jnp.int32)[None, None, :]
    ranking = jnp.argsort(logit_scores, axis=-1)[..., :MAXB - 1].astype(jnp.int32)
    offsets = jnp.concatenate((jnp.zeros((HEADS, NQB, 1), jnp.int32), ranking + 1), axis=-1)
    return ((jnp.arange(NQB, dtype=jnp.int32)[None, :, None] + offsets) % NQB).astype(jnp.int32)


def draw_block_counts(key, part):
    is_heavy = jax.random.randint(jax.random.fold_in(key, 22), (HEADS,), 0, 4) == 0
    chosen = jax.random.randint(jax.random.fold_in(key, 23), (), 0, HEADS)
    is_heavy = is_heavy | (jnp.arange(HEADS, dtype=jnp.int32) == chosen)
    high_counts = jax.random.randint(jax.random.fold_in(key, 24), (HEADS, NQB), MAXB // 2, MAXB + 1)
    low_counts = jax.random.randint(jax.random.fold_in(key, 25), (HEADS, NQB), 1, max(1, MAXB // 4) + 1)
    counts = jnp.where(is_heavy[:, None], high_counts, low_counts)
    full_row = jax.random.randint(jax.random.fold_in(key, 26), (HEADS,), 0, NQB)
    filled = is_heavy[:, None] & (jnp.arange(NQB, dtype=jnp.int32)[None, :] == full_row[:, None])
    return jnp.where(filled, MAXB, counts).astype(jnp.int32)


def shard_levels(own_key, extent, cuts, low, top_value):
    loudness, own = 1.0, jax.random.fold_in(own_key, 6)
    for dim, parts in cuts:
        heights = jnp.exp(jax.random.uniform(jax.random.fold_in(own, dim), (parts,), jnp.float32, low / len(cuts), top_value / len(cuts)))
        loudness = loudness * jnp.repeat(heights, extent[dim] // parts).reshape([-1 if axis == dim else 1 for axis in range(len(extent))])
    return loudness


def scatter_about(stream_key, shape, deviation, limit, split=(), kind=jnp.bfloat16):
    factor_of = shard_levels(stream_key, shape, split, -0.22, 0.18) if split else 1.0
    drawn = jax.random.normal(stream_key, shape, jnp.float32) * deviation * factor_of
    return jnp.minimum(jnp.maximum(drawn, -limit), limit).astype(kind)


def setup_inputs(seed: int = 0, part: int = 0) -> dict:
    arg_keys = jax.random.split(jax.random.key(seed), 6)
    part_keys = jax.random.split(jax.random.fold_in(arg_keys[5], part), 6)
    return {
        "queries": draw_queries(jax.random.fold_in(jax.random.fold_in(arg_keys[5], part), 71), part),
        "keys": draw_keys(jax.random.fold_in(jax.random.fold_in(arg_keys[5], part), 71), part),
        "values": scatter_about(part_keys[2], (TOKENS, HEADS * HEAD_FEATURES), 1.0, 6.0, ((0, 16),)),
        "block_lists": draw_block_lists(jax.random.fold_in(jax.random.fold_in(arg_keys[5], part), 71), part),
        "block_counts": draw_block_counts(jax.random.fold_in(jax.random.fold_in(arg_keys[5], part), 71), part),
    }


def one_head(operands):
    head_queries, head_keys, head_values, lists, counts = operands
    query_groups_tiled = head_queries.astype(jnp.float32).reshape(NQB, BLOCK, HEAD_FEATURES)
    key_table = head_keys.astype(jnp.float32).reshape(NQB, BLOCK, HEAD_FEATURES)
    value_table = head_values.astype(jnp.float32).reshape(NQB, BLOCK, HEAD_FEATURES)
    selected_keys = key_table[lists]
    selected_values = value_table[lists]
    logit_scores = jnp.einsum('wmi,wvui->wmvu', query_groups_tiled, selected_keys) * (1.0 / math.sqrt(HEAD_FEATURES))
    valid = jnp.arange(MAXB, dtype=jnp.int32)[None, :] < counts[:, None]
    logit_scores = jnp.where(valid[:, None, :, None], logit_scores, -jnp.inf)
    row_max = lax.optimization_barrier(jnp.max(logit_scores, axis=(2, 3), keepdims=True))
    weights = jnp.exp(logit_scores - row_max)
    row_total = lax.optimization_barrier(jnp.sum(weights, axis=(2, 3)))
    rounded_probs = lax.optimization_barrier(weights.astype(jnp.bfloat16)).astype(jnp.float32)
    weighted_sum = jnp.einsum('smlz,slzc->smc', rounded_probs, selected_values)
    result = weighted_sum / row_total[..., None]
    return result.reshape(TOKENS, HEAD_FEATURES).astype(jnp.bfloat16)

def reference(queries, keys, values, block_lists, block_counts):

    def split_heads(array):
        return array.reshape(TOKENS, HEADS, HEAD_FEATURES).transpose(1, 0, 2)
    per_head = lax.map(one_head, (split_heads(queries), split_heads(keys), split_heads(values), block_lists, block_counts))
    return per_head.transpose(1, 0, 2).reshape(TOKENS, HEADS * HEAD_FEATURES)
```

```python
import functools
import math

import jax
import jax.numpy as jnp
from jax import lax
from jax.experimental import pallas as pl
from jax.experimental.pallas import tpu as pltpu
from jax.sharding import PartitionSpec as P

BLOCK = 128


def attend_kernel(lists_ref, counts_ref, q_ref, k_ref, v_ref, o_ref, kbuf, vbuf, *, inverse_root):
    b = pl.program_id(0)
    count = counts_ref[b]
    slots = lists_ref.shape[1]
    key_blocks = k_ref.shape[0] // BLOCK
    first = lists_ref[b, 0]
    for j in range(slots):
        index = jnp.where(j < count, lists_ref[b, j], first)
        index = jnp.minimum(jnp.maximum(index, 0), key_blocks - 1)
        start = pl.multiple_of(index * BLOCK, BLOCK)
        kbuf[pl.ds(j * BLOCK, BLOCK), :] = k_ref[pl.ds(start, BLOCK), :]
        vbuf[pl.ds(j * BLOCK, BLOCK), :] = v_ref[pl.ds(start, BLOCK), :]
    logit_scores = (
        lax.dot_general(
            q_ref[...],
            kbuf[...],
            (((1,), (1,)), ((), ())),
            preferred_element_type=jnp.float32,
        )
        * inverse_root
    )
    slot_of = lax.broadcasted_iota(jnp.int32, logit_scores.shape, 1) // BLOCK
    logit_scores = jnp.where(slot_of < count, logit_scores, -jnp.inf)
    row_max = jnp.max(logit_scores, axis=1, keepdims=True)
    weights = jnp.exp(logit_scores - row_max)
    row_total = jnp.sum(weights, axis=1, keepdims=True)
    weighted_sum = jnp.dot(
        weights.astype(jnp.bfloat16), vbuf[...], preferred_element_type=jnp.float32
    )
    o_ref[...] = (weighted_sum / row_total).astype(o_ref.dtype)


def attend(head_queries, key_rows, value_rows, lists, counts):
    rows, head_size = head_queries.shape
    query_blocks = rows // BLOCK
    slots = lists.shape[1]
    key_rows_total = key_rows.shape[0]
    kernel = functools.partial(attend_kernel, inverse_root=1.0 / math.sqrt(head_size))
    grid_spec = pltpu.PrefetchScalarGridSpec(
        num_scalar_prefetch=2,
        grid=(query_blocks,),
        in_specs=[
            pl.BlockSpec((BLOCK, head_size), lambda b, lists, counts: (b, 0)),
            pl.BlockSpec((key_rows_total, head_size), lambda b, lists, counts: (0, 0)),
            pl.BlockSpec((key_rows_total, head_size), lambda b, lists, counts: (0, 0)),
        ],
        out_specs=pl.BlockSpec((BLOCK, head_size), lambda b, lists, counts: (b, 0)),
        scratch_shapes=[
            pltpu.VMEM((slots * BLOCK, head_size), head_queries.dtype),
            pltpu.VMEM((slots * BLOCK, head_size), head_queries.dtype),
        ],
    )
    return pl.pallas_call(
        kernel,
        grid_spec=grid_spec,
        out_shape=jax.ShapeDtypeStruct((rows, head_size), jnp.bfloat16),
        compiler_params=pltpu.CompilerParams(dimension_semantics=("arbitrary",)),
    )(lists, counts, head_queries, key_rows, value_rows)


def per_device(queries, keys, values, block_lists, block_counts):
    head_queries, head_keys, head_values = (
        lax.all_to_all(queries, "wide", split_axis=1, concat_axis=0, tiled=True),
        lax.all_to_all(keys, "wide", split_axis=1, concat_axis=0, tiled=True),
        lax.all_to_all(values, "wide", split_axis=1, concat_axis=0, tiled=True),
    )
    key_rows, value_rows = (
        lax.all_gather(head_keys, "narrow", axis=0, tiled=True),
        lax.all_gather(head_values, "narrow", axis=0, tiled=True),
    )
    attended = attend(head_queries, key_rows, value_rows, block_lists[0], block_counts[0])
    return lax.all_to_all(attended, "wide", split_axis=0, concat_axis=1, tiled=True)


def solution(mesh):
    in_specs = (
        P(("groups", "narrow", "wide"), None),
        P(("groups", "narrow", "wide"), None),
        P(("groups", "narrow", "wide"), None),
        P(("groups", "wide"), "narrow", None),
        P(("groups", "wide"), "narrow"),
    )
    out_specs = P(("groups", "narrow", "wide"), None)
    return jax.shard_map(
        per_device, mesh=mesh, in_specs=in_specs, out_specs=out_specs, check_vma=False
    )
```

```python
import functools
import math

import jax
import jax.numpy as jnp
from jax import lax
from jax.experimental import pallas as pl
from jax.experimental.pallas import tpu as pltpu
from jax.sharding import PartitionSpec as P

BLOCK = 128


def attend_kernel(
    lists_ref, counts_ref, q_ref, own_ref, other_ref, o_ref, kbuf, vbuf, *, inverse_root, head_size
):
    b = pl.program_id(0)
    count = counts_ref[b]
    slots = lists_ref.shape[1]
    half_blocks = other_ref.shape[0] // BLOCK
    first = lists_ref[b, 0]
    own_k = own_ref.shape[1] - 2 * head_size
    for j in range(slots):
        index = jnp.where(j < count, lists_ref[b, j], first)
        index = jnp.minimum(jnp.maximum(index, 0), 2 * half_blocks - 1)
        rows = pl.ds(j * BLOCK, BLOCK)

        @pl.when(index < half_blocks)
        def _():
            start = pl.multiple_of(index * BLOCK, BLOCK)
            kbuf[rows, :] = own_ref[pl.ds(start, BLOCK), pl.ds(own_k, head_size)]
            vbuf[rows, :] = own_ref[pl.ds(start, BLOCK), pl.ds(own_k + head_size, head_size)]

        @pl.when(index >= half_blocks)
        def _():
            start = pl.multiple_of((index - half_blocks) * BLOCK, BLOCK)
            kbuf[rows, :] = other_ref[pl.ds(start, BLOCK), pl.ds(0, head_size)]
            vbuf[rows, :] = other_ref[pl.ds(start, BLOCK), pl.ds(head_size, head_size)]

    logit_scores = (
        lax.dot_general(
            q_ref[...],
            kbuf[...],
            (((1,), (1,)), ((), ())),
            preferred_element_type=jnp.float32,
        )
        * inverse_root
    )
    slot_of = lax.broadcasted_iota(jnp.int32, logit_scores.shape, 1) // BLOCK
    logit_scores = jnp.where(slot_of < count, logit_scores, -jnp.inf)
    row_max = jnp.max(logit_scores, axis=1, keepdims=True)
    weights = jnp.exp(logit_scores - row_max)
    row_total = jnp.sum(weights, axis=1, keepdims=True)
    weighted_sum = jnp.dot(
        weights.astype(jnp.bfloat16), vbuf[...], preferred_element_type=jnp.float32
    )
    o_ref[...] = (weighted_sum / row_total).astype(o_ref.dtype)


def attend(own, other, lists, counts, head_size):
    rows = own.shape[0]
    query_blocks = rows // BLOCK
    slots = lists.shape[1]
    kernel = functools.partial(
        attend_kernel, inverse_root=1.0 / math.sqrt(head_size), head_size=head_size
    )
    grid_spec = pltpu.PrefetchScalarGridSpec(
        num_scalar_prefetch=2,
        grid=(query_blocks,),
        in_specs=[
            pl.BlockSpec((BLOCK, head_size), lambda b, lists, counts: (b, 0)),
            pl.BlockSpec(own.shape, lambda b, lists, counts: (0, 0)),
            pl.BlockSpec(other.shape, lambda b, lists, counts: (0, 0)),
        ],
        out_specs=pl.BlockSpec((BLOCK, head_size), lambda b, lists, counts: (b, 0)),
        scratch_shapes=[
            pltpu.VMEM((slots * BLOCK, head_size), own.dtype),
            pltpu.VMEM((slots * BLOCK, head_size), own.dtype),
        ],
    )
    return pl.pallas_call(
        kernel,
        grid_spec=grid_spec,
        out_shape=jax.ShapeDtypeStruct((rows, head_size), jnp.bfloat16),
        compiler_params=pltpu.CompilerParams(dimension_semantics=("arbitrary",)),
    )(lists, counts, own, own, other)


def per_device(queries, keys, values, block_lists, block_counts):
    rows = queries.shape[0]
    width = lax.axis_size("wide")
    head_size = queries.shape[1] // width
    stacked = jnp.concatenate(
        [a.reshape(rows, width, head_size) for a in (queries, keys, values)], axis=2
    )
    own = lax.all_to_all(stacked, "wide", split_axis=1, concat_axis=0, tiled=True)
    own = own.reshape(rows * width, 3 * head_size)
    other = lax.ppermute(own[:, head_size:], "narrow", [(0, 1), (1, 0)])
    half_blocks = own.shape[0] // BLOCK
    n = lax.axis_index("narrow")
    lists = (block_lists[0] + (2 * half_blocks - n * half_blocks)) % (2 * half_blocks)
    attended = attend(own, other, lists, block_counts[0], head_size)
    return lax.all_to_all(attended, "wide", split_axis=0, concat_axis=1, tiled=True)


def solution(mesh):
    in_specs = (
        P(("groups", "narrow", "wide"), None),
        P(("groups", "narrow", "wide"), None),
        P(("groups", "narrow", "wide"), None),
        P(("groups", "wide"), "narrow", None),
        P(("groups", "wide"), "narrow"),
    )
    out_specs = P(("groups", "narrow", "wide"), None)
    return jax.shard_map(
        per_device, mesh=mesh, in_specs=in_specs, out_specs=out_specs, check_vma=False
    )
```

```python
import functools
import math

import jax
import jax.numpy as jnp
from jax import lax
from jax.experimental import pallas as pl
from jax.experimental.pallas import tpu as pltpu
from jax.sharding import PartitionSpec as P

BLOCK = 128
CHUNK = 4


def attend_kernel(
    lists_ref, counts_ref, own_ref, other_ref, o_ref, kbuf, vbuf, sbuf, *, inverse_root, head_size
):
    query_blocks = own_ref.shape[0] // BLOCK
    slots = lists_ref.shape[1]
    half_blocks = other_ref.shape[0] // BLOCK
    own_k = own_ref.shape[1] - 2 * head_size
    chunk_keys = CHUNK * BLOCK

    def one_block(b, carry):
        count = counts_ref[b]
        chunks = (count + (CHUNK - 1)) // CHUNK
        first = lists_ref[b, 0]
        for j in range(slots):
            index = jnp.where(j < count, lists_ref[b, j], first)
            index = jnp.minimum(jnp.maximum(index, 0), 2 * half_blocks - 1)
            rows = pl.ds((j % CHUNK) * BLOCK, BLOCK)
            live = j < chunks * CHUNK

            @pl.when(live & (index < half_blocks))
            def _():
                start = pl.multiple_of(index * BLOCK, BLOCK)
                kbuf[j // CHUNK, rows, :] = own_ref[pl.ds(start, BLOCK), pl.ds(own_k, head_size)]
                vbuf[j // CHUNK, rows, :] = own_ref[
                    pl.ds(start, BLOCK), pl.ds(own_k + head_size, head_size)
                ]

            @pl.when(live & (index >= half_blocks))
            def _():
                start = pl.multiple_of((index - half_blocks) * BLOCK, BLOCK)
                kbuf[j // CHUNK, rows, :] = other_ref[pl.ds(start, BLOCK), pl.ds(0, head_size)]
                vbuf[j // CHUNK, rows, :] = other_ref[
                    pl.ds(start, BLOCK), pl.ds(head_size, head_size)
                ]

        q_rows = pl.ds(pl.multiple_of(b * BLOCK, BLOCK), BLOCK)
        queries = own_ref[q_rows, pl.ds(0, head_size)]

        def scores_pass(c, row_max):
            logit_scores = (
                lax.dot_general(
                    queries,
                    kbuf[c],
                    (((1,), (1,)), ((), ())),
                    preferred_element_type=jnp.float32,
                )
                * inverse_root
            )
            sbuf[c] = logit_scores
            return jnp.maximum(row_max, jnp.max(logit_scores, axis=1, keepdims=True))

        row_max = lax.fori_loop(
            0, chunks, scores_pass, jnp.full((BLOCK, 1), -jnp.inf, jnp.float32)
        )

        def weights_pass(c, carry):
            row_total, weighted_sum = carry
            weights = jnp.exp(sbuf[c] - row_max)
            slot_of = c * CHUNK + lax.broadcasted_iota(jnp.int32, weights.shape, 1) // BLOCK
            weights = jnp.where(slot_of < count, weights, 0.0)
            row_total = row_total + jnp.sum(weights, axis=1, keepdims=True)
            weighted_sum = weighted_sum + jnp.dot(
                weights.astype(jnp.bfloat16), vbuf[c], preferred_element_type=jnp.float32
            )
            return row_total, weighted_sum

        row_total, weighted_sum = lax.fori_loop(
            0,
            chunks,
            weights_pass,
            (
                jnp.zeros((BLOCK, 1), jnp.float32),
                jnp.zeros((BLOCK, head_size), jnp.float32),
            ),
        )
        o_ref[q_rows, :] = (weighted_sum / row_total).astype(o_ref.dtype)
        return carry

    lax.fori_loop(0, query_blocks, one_block, 0)


def attend(own, other, lists, counts, head_size):
    rows = own.shape[0]
    slots = lists.shape[1]
    chunks = -(-slots // CHUNK)
    kernel = functools.partial(
        attend_kernel, inverse_root=1.0 / math.sqrt(head_size), head_size=head_size
    )
    grid_spec = pltpu.PrefetchScalarGridSpec(
        num_scalar_prefetch=2,
        grid=(1,),
        in_specs=[
            pl.BlockSpec(own.shape, lambda i, lists, counts: (0, 0)),
            pl.BlockSpec(other.shape, lambda i, lists, counts: (0, 0)),
        ],
        out_specs=pl.BlockSpec((rows, head_size), lambda i, lists, counts: (0, 0)),
        scratch_shapes=[
            pltpu.VMEM((chunks, CHUNK * BLOCK, head_size), own.dtype),
            pltpu.VMEM((chunks, CHUNK * BLOCK, head_size), own.dtype),
            pltpu.VMEM((chunks, BLOCK, CHUNK * BLOCK), jnp.float32),
        ],
    )
    return pl.pallas_call(
        kernel,
        grid_spec=grid_spec,
        out_shape=jax.ShapeDtypeStruct((rows, head_size), jnp.bfloat16),
        compiler_params=pltpu.CompilerParams(dimension_semantics=("arbitrary",)),
    )(lists, counts, own, other)


def per_device(queries, keys, values, block_lists, block_counts):
    rows = queries.shape[0]
    width = lax.axis_size("wide")
    head_size = queries.shape[1] // width
    stacked = jnp.concatenate(
        [a.reshape(rows, width, head_size) for a in (queries, keys, values)], axis=2
    )
    own = lax.all_to_all(stacked, "wide", split_axis=1, concat_axis=0, tiled=True)
    own = own.reshape(rows * width, 3 * head_size)
    other = lax.ppermute(own[:, head_size:], "narrow", [(0, 1), (1, 0)])
    half_blocks = own.shape[0] // BLOCK
    n = lax.axis_index("narrow")
    lists = (block_lists[0] + (2 * half_blocks - n * half_blocks)) % (2 * half_blocks)
    attended = attend(own, other, lists, block_counts[0], head_size)
    return lax.all_to_all(attended, "wide", split_axis=0, concat_axis=1, tiled=True)


def solution(mesh):
    in_specs = (
        P(("groups", "narrow", "wide"), None),
        P(("groups", "narrow", "wide"), None),
        P(("groups", "narrow", "wide"), None),
        P(("groups", "wide"), "narrow", None),
        P(("groups", "wide"), "narrow"),
    )
    out_specs = P(("groups", "narrow", "wide"), None)
    return jax.shard_map(
        per_device, mesh=mesh, in_specs=in_specs, out_specs=out_specs, check_vma=False
    )
```

```python
import functools
import math

import jax
import jax.numpy as jnp
from jax import lax
from jax.experimental import pallas as pl
from jax.experimental.pallas import tpu as pltpu
from jax.sharding import PartitionSpec as P

BLOCK = 128
SUBLANES = 8


def attend_kernel(
    lists_ref,
    counts_ref,
    narrow_ref,
    q_ref,
    own_ref,
    other_ref,
    o_ref,
    table,
    kbuf,
    vbuf,
    mask,
    sems,
    *,
    inverse_root,
    head_size,
):
    b = pl.program_id(0)
    half_rows = other_ref.shape[0]
    n = narrow_ref[0]

    @pl.when(b == 0)
    def _():
        own_copy = pltpu.make_async_copy(
            own_ref.at[:, pl.ds(head_size, 2 * head_size)],
            table.at[pl.ds(n * half_rows, half_rows), :],
            sems.at[0],
        )
        other_copy = pltpu.make_async_copy(
            other_ref, table.at[pl.ds((1 - n) * half_rows, half_rows), :], sems.at[1]
        )
        own_copy.start()
        other_copy.start()
        own_copy.wait()
        other_copy.wait()

    count = counts_ref[b]
    slots = lists_ref.shape[1]
    key_blocks = table.shape[0] // BLOCK
    first = lists_ref[b, 0]
    for j in range(slots):
        index = jnp.where(j < count, lists_ref[b, j], first)
        index = jnp.minimum(jnp.maximum(index, 0), key_blocks - 1)
        start = pl.multiple_of(index * BLOCK, BLOCK)
        kbuf[pl.ds(j * BLOCK, BLOCK), :] = table[pl.ds(start, BLOCK), pl.ds(0, head_size)]
        vbuf[pl.ds(j * BLOCK, BLOCK), :] = table[pl.ds(start, BLOCK), pl.ds(head_size, head_size)]
    slot_of = lax.broadcasted_iota(jnp.int32, mask.shape, 1) // BLOCK
    mask[...] = jnp.where(slot_of < count, 1.0, 0.0).astype(mask.dtype)

    logit_scores = (
        lax.dot_general(
            q_ref[...],
            kbuf[...],
            (((1,), (1,)), ((), ())),
            preferred_element_type=jnp.float32,
        )
        * inverse_root
    )
    row_max = jnp.max(logit_scores, axis=1, keepdims=True)
    weights = jnp.exp(logit_scores - row_max)
    width = weights.shape[1]
    weights = (weights.reshape(-1, SUBLANES, width) * mask[...]).reshape(-1, width)
    row_total = jnp.sum(weights, axis=1, keepdims=True)
    weighted_sum = jnp.dot(
        weights.astype(jnp.bfloat16), vbuf[...], preferred_element_type=jnp.float32
    )
    o_ref[...] = (weighted_sum / row_total).astype(o_ref.dtype)


def attend(own, other, lists, counts, narrow, head_size):
    rows = own.shape[0]
    query_blocks = rows // BLOCK
    slots = lists.shape[1]
    kernel = functools.partial(
        attend_kernel, inverse_root=1.0 / math.sqrt(head_size), head_size=head_size
    )
    grid_spec = pltpu.PrefetchScalarGridSpec(
        num_scalar_prefetch=3,
        grid=(query_blocks,),
        in_specs=[
            pl.BlockSpec((BLOCK, head_size), lambda b, *_: (b, 0)),
            pl.BlockSpec(memory_space=pl.ANY),
            pl.BlockSpec(memory_space=pl.ANY),
        ],
        out_specs=pl.BlockSpec((BLOCK, head_size), lambda b, *_: (b, 0)),
        scratch_shapes=[
            pltpu.VMEM((2 * other.shape[0], 2 * head_size), own.dtype),
            pltpu.VMEM((slots * BLOCK, head_size), own.dtype),
            pltpu.VMEM((slots * BLOCK, head_size), own.dtype),
            pltpu.VMEM((SUBLANES, slots * BLOCK), jnp.float32),
            pltpu.SemaphoreType.DMA((2,)),
        ],
    )
    return pl.pallas_call(
        kernel,
        grid_spec=grid_spec,
        out_shape=jax.ShapeDtypeStruct((rows, head_size), jnp.bfloat16),
        compiler_params=pltpu.CompilerParams(dimension_semantics=("arbitrary",)),
    )(lists, counts, narrow, own, own, other)


def per_device(queries, keys, values, block_lists, block_counts):
    rows = queries.shape[0]
    width = lax.axis_size("wide")
    head_size = queries.shape[1] // width
    stacked = jnp.concatenate(
        [a.reshape(rows, width, head_size) for a in (queries, keys, values)], axis=2
    )
    own = lax.all_to_all(stacked, "wide", split_axis=1, concat_axis=0, tiled=True)
    own = own.reshape(rows * width, 3 * head_size)
    other = lax.ppermute(own[:, head_size:], "narrow", [(0, 1), (1, 0)])
    narrow = lax.axis_index("narrow").astype(jnp.int32).reshape(1)
    attended = attend(own, other, block_lists[0], block_counts[0], narrow, head_size)
    return lax.all_to_all(attended, "wide", split_axis=0, concat_axis=1, tiled=True)


def solution(mesh):
    in_specs = (
        P(("groups", "narrow", "wide"), None),
        P(("groups", "narrow", "wide"), None),
        P(("groups", "narrow", "wide"), None),
        P(("groups", "wide"), "narrow", None),
        P(("groups", "wide"), "narrow"),
    )
    out_specs = P(("groups", "narrow", "wide"), None)
    return jax.shard_map(
        per_device, mesh=mesh, in_specs=in_specs, out_specs=out_specs, check_vma=False
    )
```

```python
import functools
import math

import jax
import jax.numpy as jnp
from jax import lax
from jax.experimental import pallas as pl
from jax.experimental.pallas import tpu as pltpu
from jax.sharding import PartitionSpec as P

BLOCK = 128
SUBLANES = 8


def attend_kernel(
    lists_ref,
    counts_ref,
    narrow_ref,
    order_ref,
    q_ref,
    own_ref,
    other_ref,
    o_ref,
    table,
    kbuf,
    vbuf,
    mask,
    sems,
    *,
    inverse_root,
    head_size,
):
    step = pl.program_id(0)
    b = order_ref[step]
    half_rows = other_ref.shape[0]
    n = narrow_ref[0]

    @pl.when(step == 0)
    def _():
        own_copy = pltpu.make_async_copy(
            own_ref.at[:, pl.ds(head_size, 2 * head_size)],
            table.at[pl.ds(n * half_rows, half_rows), :],
            sems.at[0],
        )
        other_copy = pltpu.make_async_copy(
            other_ref, table.at[pl.ds((1 - n) * half_rows, half_rows), :], sems.at[1]
        )
        own_copy.start()
        other_copy.start()
        own_copy.wait()
        other_copy.wait()

    count = counts_ref[b]
    slots = lists_ref.shape[1]
    key_blocks = table.shape[0] // BLOCK
    first = lists_ref[b, 0]
    for j in range(slots):
        index = jnp.where(j < count, lists_ref[b, j], first)
        index = jnp.minimum(jnp.maximum(index, 0), key_blocks - 1)
        start = pl.multiple_of(index * BLOCK, BLOCK)
        kbuf[pl.ds(j * BLOCK, BLOCK), :] = table[pl.ds(start, BLOCK), pl.ds(0, head_size)]
        vbuf[pl.ds(j * BLOCK, BLOCK), :] = table[pl.ds(start, BLOCK), pl.ds(head_size, head_size)]
    slot_of = lax.broadcasted_iota(jnp.int32, mask.shape, 1) // BLOCK
    mask[...] = jnp.where(slot_of < count, 1.0, 0.0).astype(mask.dtype)

    logit_scores = (
        lax.dot_general(
            q_ref[...],
            kbuf[...],
            (((1,), (1,)), ((), ())),
            preferred_element_type=jnp.float32,
        )
        * inverse_root
    )
    row_max = jnp.max(logit_scores, axis=1, keepdims=True)
    weights = jnp.exp(logit_scores - row_max)
    width = weights.shape[1]
    weights = (weights.reshape(-1, SUBLANES, width) * mask[...]).reshape(-1, width)
    row_total = jnp.sum(weights, axis=1, keepdims=True)
    weighted_sum = jnp.dot(
        weights.astype(jnp.bfloat16), vbuf[...], preferred_element_type=jnp.float32
    )
    o_ref[...] = (weighted_sum / row_total).astype(o_ref.dtype)


def attend(own, other, lists, counts, narrow, order, head_size):
    query_blocks = order.shape[0]
    rows = query_blocks * BLOCK
    slots = lists.shape[1]
    kernel = functools.partial(
        attend_kernel, inverse_root=1.0 / math.sqrt(head_size), head_size=head_size
    )
    grid_spec = pltpu.PrefetchScalarGridSpec(
        num_scalar_prefetch=4,
        grid=(query_blocks,),
        in_specs=[
            pl.BlockSpec((BLOCK, head_size), lambda b, lists, counts, narrow, order: (order[b], 0)),
            pl.BlockSpec(memory_space=pl.ANY),
            pl.BlockSpec(memory_space=pl.ANY),
        ],
        out_specs=pl.BlockSpec((BLOCK, head_size), lambda b, *_: (b, 0)),
        scratch_shapes=[
            pltpu.VMEM((2 * other.shape[0], 2 * head_size), own.dtype),
            pltpu.VMEM((slots * BLOCK, head_size), own.dtype),
            pltpu.VMEM((slots * BLOCK, head_size), own.dtype),
            pltpu.VMEM((SUBLANES, slots * BLOCK), jnp.float32),
            pltpu.SemaphoreType.DMA((2,)),
        ],
    )
    return pl.pallas_call(
        kernel,
        grid_spec=grid_spec,
        out_shape=jax.ShapeDtypeStruct((rows, head_size), jnp.bfloat16),
        compiler_params=pltpu.CompilerParams(dimension_semantics=("arbitrary",)),
        cost_estimate=pl.CostEstimate(
            flops=4 * rows * slots * BLOCK * head_size,
            transcendentals=rows * slots * BLOCK,
            bytes_accessed=2 * other.size * other.dtype.itemsize + 2 * rows * head_size * 2,
        ),
    )(lists, counts, narrow, order, own, own, other)


def per_device(queries, keys, values, block_lists, block_counts):
    rows = queries.shape[0]
    width = lax.axis_size("wide")
    head_size = queries.shape[1] // width
    stacked = jnp.concatenate(
        [a.reshape(rows, width, head_size) for a in (queries, keys, values)], axis=2
    )
    own = lax.all_to_all(stacked, "wide", split_axis=1, concat_axis=0, tiled=True)
    own = own.reshape(rows * width, 3 * head_size)
    other = lax.ppermute(own[:, head_size:], "narrow", [(0, 1), (1, 0)])
    narrow = lax.axis_index("narrow").astype(jnp.int32).reshape(1)
    w = lax.axis_index("wide").astype(jnp.int32)
    chunk_blocks = rows // BLOCK
    shifts = list(range(1, width)) + [0]
    early = shifts[: width // 2]
    late = shifts[width // 2 :]

    def block_order(group):
        group_shifts = jnp.array(group, jnp.int32)
        dest = (w + group_shifts) % width
        return (dest[:, None] * chunk_blocks + jnp.arange(chunk_blocks, dtype=jnp.int32)).reshape(-1)

    received = [None] * width
    for group in (early, late):
        attended = attend(
            own, other, block_lists[0], block_counts[0], narrow, block_order(group), head_size
        )
        for i, s in enumerate(group):
            chunk = attended[i * rows : (i + 1) * rows]
            if s:
                chunk = lax.ppermute(chunk, "wide", [(d, (d + s) % width) for d in range(width)])
            received[s] = chunk
    by_source = jnp.stack(received)
    sources = (w - jnp.arange(width, dtype=jnp.int32)) % width
    placed = jnp.zeros_like(by_source).at[sources].set(by_source)
    return placed.transpose(1, 0, 2).reshape(rows, width * head_size)


def solution(mesh):
    in_specs = (
        P(("groups", "narrow", "wide"), None),
        P(("groups", "narrow", "wide"), None),
        P(("groups", "narrow", "wide"), None),
        P(("groups", "wide"), "narrow", None),
        P(("groups", "wide"), "narrow"),
    )
    out_specs = P(("groups", "narrow", "wide"), None)
    return jax.shard_map(
        per_device, mesh=mesh, in_specs=in_specs, out_specs=out_specs, check_vma=False
    )
```

```python
import functools
import math

import jax
import jax.numpy as jnp
from jax import lax
from jax.experimental import pallas as pl
from jax.experimental.pallas import tpu as pltpu
from jax.sharding import PartitionSpec as P

BLOCK = 128
SUBLANES = 8
GROUP = 8


def attend_kernel(
    lists_ref,
    counts_ref,
    narrow_ref,
    q_ref,
    own_ref,
    other_ref,
    o_ref,
    table,
    kbuf,
    vbuf,
    mask,
    sems,
    *,
    inverse_root,
    head_size,
):
    step = pl.program_id(0)
    half_rows = other_ref.shape[0]
    n = narrow_ref[0]

    @pl.when(step == 0)
    def _():
        own_copy = pltpu.make_async_copy(
            own_ref.at[:, pl.ds(head_size, 2 * head_size)],
            table.at[pl.ds(n * half_rows, half_rows), :],
            sems.at[0],
        )
        other_copy = pltpu.make_async_copy(
            other_ref, table.at[pl.ds((1 - n) * half_rows, half_rows), :], sems.at[1]
        )
        own_copy.start()
        other_copy.start()
        own_copy.wait()
        other_copy.wait()

    group = q_ref.shape[0] // BLOCK
    slots = lists_ref.shape[1]
    key_blocks = table.shape[0] // BLOCK
    for g in range(group):
        b = step * group + g
        count = counts_ref[b]
        first = lists_ref[b, 0]
        for j in range(slots):
            index = jnp.where(j < count, lists_ref[b, j], first)
            index = jnp.minimum(jnp.maximum(index, 0), key_blocks - 1)
            start = pl.multiple_of(index * BLOCK, BLOCK)
            kbuf[g, pl.ds(j * BLOCK, BLOCK), :] = table[pl.ds(start, BLOCK), pl.ds(0, head_size)]
            vbuf[g, pl.ds(j * BLOCK, BLOCK), :] = table[
                pl.ds(start, BLOCK), pl.ds(head_size, head_size)
            ]
        slot_of = lax.broadcasted_iota(jnp.int32, mask.shape[1:], 1) // BLOCK
        mask[g] = jnp.where(slot_of < count, 1.0, 0.0).astype(mask.dtype)

    for g in range(group):
        rows = pl.ds(g * BLOCK, BLOCK)
        logit_scores = (
            lax.dot_general(
                q_ref[rows, :],
                kbuf[g],
                (((1,), (1,)), ((), ())),
                preferred_element_type=jnp.float32,
            )
            * inverse_root
        )
        row_max = jnp.max(logit_scores, axis=1, keepdims=True)
        weights = jnp.exp(logit_scores - row_max)
        width = weights.shape[1]
        weights = (weights.reshape(-1, SUBLANES, width) * mask[g]).reshape(-1, width)
        row_total = jnp.sum(weights, axis=1, keepdims=True)
        weighted_sum = jnp.dot(
            weights.astype(jnp.bfloat16), vbuf[g], preferred_element_type=jnp.float32
        )
        o_ref[rows, :] = (weighted_sum / row_total).astype(o_ref.dtype)


def attend(own, other, lists, counts, narrow, head_size):
    rows = own.shape[0]
    query_blocks = rows // BLOCK
    group = max(g for g in range(1, GROUP + 1) if query_blocks % g == 0)
    slots = lists.shape[1]
    kernel = functools.partial(
        attend_kernel, inverse_root=1.0 / math.sqrt(head_size), head_size=head_size
    )
    grid_spec = pltpu.PrefetchScalarGridSpec(
        num_scalar_prefetch=3,
        grid=(query_blocks // group,),
        in_specs=[
            pl.BlockSpec((group * BLOCK, head_size), lambda b, *_: (b, 0)),
            pl.BlockSpec(memory_space=pl.ANY),
            pl.BlockSpec(memory_space=pl.ANY),
        ],
        out_specs=pl.BlockSpec((group * BLOCK, head_size), lambda b, *_: (b, 0)),
        scratch_shapes=[
            pltpu.VMEM((2 * other.shape[0], 2 * head_size), own.dtype),
            pltpu.VMEM((group, slots * BLOCK, head_size), own.dtype),
            pltpu.VMEM((group, slots * BLOCK, head_size), own.dtype),
            pltpu.VMEM((group, SUBLANES, slots * BLOCK), jnp.float32),
            pltpu.SemaphoreType.DMA((2,)),
        ],
    )
    return pl.pallas_call(
        kernel,
        grid_spec=grid_spec,
        out_shape=jax.ShapeDtypeStruct((rows, head_size), jnp.bfloat16),
        compiler_params=pltpu.CompilerParams(dimension_semantics=("arbitrary",)),
    )(lists, counts, narrow, own, own, other)


def per_device(queries, keys, values, block_lists, block_counts):
    rows = queries.shape[0]
    width = lax.axis_size("wide")
    head_size = queries.shape[1] // width
    stacked = jnp.concatenate(
        [a.reshape(rows, width, head_size) for a in (queries, keys, values)], axis=2
    )
    own = lax.all_to_all(stacked, "wide", split_axis=1, concat_axis=0, tiled=True)
    own = own.reshape(rows * width, 3 * head_size)
    other = lax.ppermute(own[:, head_size:], "narrow", [(0, 1), (1, 0)])
    narrow = lax.axis_index("narrow").astype(jnp.int32).reshape(1)
    attended = attend(own, other, block_lists[0], block_counts[0], narrow, head_size)
    return lax.all_to_all(attended, "wide", split_axis=0, concat_axis=1, tiled=True)


def solution(mesh):
    in_specs = (
        P(("groups", "narrow", "wide"), None),
        P(("groups", "narrow", "wide"), None),
        P(("groups", "narrow", "wide"), None),
        P(("groups", "wide"), "narrow", None),
        P(("groups", "wide"), "narrow"),
    )
    out_specs = P(("groups", "narrow", "wide"), None)
    return jax.shard_map(
        per_device, mesh=mesh, in_specs=in_specs, out_specs=out_specs, check_vma=False
    )
```

```python
import functools
import math

import jax
import numpy as np
import jax.numpy as jnp
from jax import lax
from jax.experimental import pallas as pl
from jax.experimental.pallas import tpu as pltpu
from jax.sharding import PartitionSpec as P

BLOCK = 128
SUBLANES = 8
GROUP = 8


def attend_kernel(
    lists_ref,
    counts_ref,
    narrow_ref,
    order_ref,
    q_ref,
    own_ref,
    other_ref,
    o_ref,
    table,
    kbuf,
    vbuf,
    mask,
    sems,
    *,
    inverse_root,
    head_size,
):
    step = pl.program_id(0)
    half_rows = other_ref.shape[0]
    n = narrow_ref[0]

    @pl.when(step == 0)
    def _():
        own_copy = pltpu.make_async_copy(
            own_ref.at[:, pl.ds(head_size, 2 * head_size)],
            table.at[pl.ds(n * half_rows, half_rows), :],
            sems.at[0],
        )
        other_copy = pltpu.make_async_copy(
            other_ref, table.at[pl.ds((1 - n) * half_rows, half_rows), :], sems.at[1]
        )
        own_copy.start()
        other_copy.start()
        own_copy.wait()
        other_copy.wait()

    group = o_ref.shape[0] // BLOCK
    slots = lists_ref.shape[1]
    key_blocks = table.shape[0] // BLOCK
    for g in range(group):
        b = order_ref[step * group + g]
        count = counts_ref[b]
        first = lists_ref[b, 0]
        for j in range(slots):
            index = jnp.where(j < count, lists_ref[b, j], first)
            index = jnp.minimum(jnp.maximum(index, 0), key_blocks - 1)
            start = pl.multiple_of(index * BLOCK, BLOCK)
            kbuf[g, pl.ds(j * BLOCK, BLOCK), :] = table[pl.ds(start, BLOCK), pl.ds(0, head_size)]
            vbuf[g, pl.ds(j * BLOCK, BLOCK), :] = table[
                pl.ds(start, BLOCK), pl.ds(head_size, head_size)
            ]
        slot_of = lax.broadcasted_iota(jnp.int32, mask.shape[1:], 1) // BLOCK
        mask[g] = jnp.where(slot_of < count, 1.0, 0.0).astype(mask.dtype)

    for g in range(group):
        rows = pl.ds(g * BLOCK, BLOCK)
        b = order_ref[step * group + g]
        q_rows = pl.ds(pl.multiple_of(b * BLOCK, BLOCK), BLOCK)
        logit_scores = (
            lax.dot_general(
                q_ref[q_rows, pl.ds(0, head_size)],
                kbuf[g],
                (((1,), (1,)), ((), ())),
                preferred_element_type=jnp.float32,
            )
            * inverse_root
        )
        row_max = jnp.max(logit_scores, axis=1, keepdims=True)
        weights = jnp.exp(logit_scores - row_max)
        width = weights.shape[1]
        weights = (weights.reshape(-1, SUBLANES, width) * mask[g]).reshape(-1, width)
        row_total = jnp.sum(weights, axis=1, keepdims=True)
        weighted_sum = jnp.dot(
            weights.astype(jnp.bfloat16), vbuf[g], preferred_element_type=jnp.float32
        )
        o_ref[rows, :] = (weighted_sum / row_total).astype(o_ref.dtype)


def attend(own, other, lists, counts, narrow, order, head_size):
    query_blocks = order.shape[0]
    rows = query_blocks * BLOCK
    group = max(g for g in range(1, GROUP + 1) if query_blocks % g == 0)
    slots = lists.shape[1]
    kernel = functools.partial(
        attend_kernel, inverse_root=1.0 / math.sqrt(head_size), head_size=head_size
    )
    grid_spec = pltpu.PrefetchScalarGridSpec(
        num_scalar_prefetch=4,
        grid=(query_blocks // group,),
        in_specs=[
            pl.BlockSpec(own.shape, lambda b, *_: (0, 0)),
            pl.BlockSpec(memory_space=pl.ANY),
            pl.BlockSpec(memory_space=pl.ANY),
        ],
        out_specs=pl.BlockSpec((group * BLOCK, head_size), lambda b, *_: (b, 0)),
        scratch_shapes=[
            pltpu.VMEM((2 * other.shape[0], 2 * head_size), own.dtype),
            pltpu.VMEM((group, slots * BLOCK, head_size), own.dtype),
            pltpu.VMEM((group, slots * BLOCK, head_size), own.dtype),
            pltpu.VMEM((group, SUBLANES, slots * BLOCK), jnp.float32),
            pltpu.SemaphoreType.DMA((2,)),
        ],
    )
    return pl.pallas_call(
        kernel,
        grid_spec=grid_spec,
        out_shape=jax.ShapeDtypeStruct((rows, head_size), jnp.bfloat16),
        compiler_params=pltpu.CompilerParams(dimension_semantics=("arbitrary",)),
    )(lists, counts, narrow, order, own, own, other)


def per_device(queries, keys, values, block_lists, block_counts):
    rows = queries.shape[0]
    width = lax.axis_size("wide")
    head_size = queries.shape[1] // width
    stacked = jnp.concatenate(
        [a.reshape(rows, width, head_size) for a in (queries, keys, values)], axis=2
    )
    own = lax.all_to_all(stacked, "wide", split_axis=1, concat_axis=0, tiled=True)
    own = own.reshape(rows * width, 3 * head_size)
    other = lax.ppermute(own[:, head_size:], "narrow", [(0, 1), (1, 0)])
    narrow = lax.axis_index("narrow").astype(jnp.int32).reshape(1)
    chunk_blocks = rows // BLOCK
    split = max(chunk_blocks // 2, 1)
    parts = []
    for part in (range(split), range(split, chunk_blocks)):
        if not len(part):
            continue
        order = (
            np.arange(width)[:, None] * chunk_blocks + np.array(list(part))[None, :]
        ).reshape(-1)
        attended = attend(
            own, other, block_lists[0], block_counts[0], narrow, jnp.asarray(order, jnp.int32),
            head_size,
        )
        attended = attended.reshape(width, len(part) * BLOCK, head_size)
        parts.append(lax.all_to_all(attended, "wide", split_axis=0, concat_axis=0, tiled=True))
    by_head = jnp.concatenate(parts, axis=1)
    return by_head.transpose(1, 0, 2).reshape(rows, width * head_size)


def solution(mesh):
    in_specs = (
        P(("groups", "narrow", "wide"), None),
        P(("groups", "narrow", "wide"), None),
        P(("groups", "narrow", "wide"), None),
        P(("groups", "wide"), "narrow", None),
        P(("groups", "wide"), "narrow"),
    )
    out_specs = P(("groups", "narrow", "wide"), None)
    return jax.shard_map(
        per_device, mesh=mesh, in_specs=in_specs, out_specs=out_specs, check_vma=False
    )
```

```python
import functools
import math

import jax
import jax.numpy as jnp
from jax import lax
from jax.experimental import pallas as pl
from jax.experimental.pallas import tpu as pltpu
from jax.sharding import PartitionSpec as P

BLOCK = 128
GROUP = 8


def attend_kernel(
    lists_ref,
    counts_ref,
    narrow_ref,
    q_ref,
    own_ref,
    other_ref,
    o_ref,
    table,
    kbuf,
    vbuf,
    sems,
    *,
    inverse_root,
    head_size,
):
    step = pl.program_id(0)
    half_rows = other_ref.shape[0]
    n = narrow_ref[0]

    @pl.when(step == 0)
    def _():
        own_copy = pltpu.make_async_copy(
            own_ref.at[:, pl.ds(head_size, 2 * head_size)],
            table.at[pl.ds(n * half_rows, half_rows), :],
            sems.at[0],
        )
        other_copy = pltpu.make_async_copy(
            other_ref, table.at[pl.ds((1 - n) * half_rows, half_rows), :], sems.at[1]
        )
        own_copy.start()
        other_copy.start()
        own_copy.wait()
        other_copy.wait()

    group = q_ref.shape[0] // BLOCK
    slots = lists_ref.shape[1]
    key_blocks = 2 * half_rows // BLOCK
    zero_block = key_blocks

    @pl.when(step == 0)
    def _():
        table[pl.ds(zero_block * BLOCK, BLOCK), :] = jnp.zeros((BLOCK, table.shape[1]), table.dtype)

    for g in range(group):
        b = step * group + g
        count = counts_ref[b]
        first = lists_ref[b, 0]
        for j in range(slots):
            index = jnp.where(j < count, lists_ref[b, j], first)
            index = jnp.minimum(jnp.maximum(index, 0), key_blocks - 1)
            value_index = jnp.where(j < count, index, zero_block)
            start = pl.multiple_of(index * BLOCK, BLOCK)
            value_start = pl.multiple_of(value_index * BLOCK, BLOCK)
            kbuf[g, pl.ds(j * BLOCK, BLOCK), :] = table[pl.ds(start, BLOCK), pl.ds(0, head_size)]
            vbuf[g, pl.ds(j * BLOCK, BLOCK), :] = table[
                pl.ds(value_start, BLOCK), pl.ds(head_size, head_size)
            ]

    exponent_scale = inverse_root * math.log2(math.e)
    for g in range(group):
        rows = pl.ds(g * BLOCK, BLOCK)
        count = counts_ref[step * group + g]
        raw_scores = lax.dot_general(
            q_ref[rows, :],
            kbuf[g],
            (((1,), (1,)), ((), ())),
            preferred_element_type=jnp.float32,
        )
        raw_max = jnp.max(raw_scores, axis=1, keepdims=True)
        weights = jnp.exp2((raw_scores - raw_max) * exponent_scale)
        padded = (slots - count).astype(jnp.float32)
        row_total = jnp.sum(weights, axis=1, keepdims=True) - padded * jnp.sum(
            weights[:, :BLOCK], axis=1, keepdims=True
        )
        weighted_sum = jnp.dot(
            weights.astype(jnp.bfloat16), vbuf[g], preferred_element_type=jnp.float32
        )
        o_ref[rows, :] = (weighted_sum / row_total).astype(o_ref.dtype)


def attend(own, other, lists, counts, narrow, head_size):
    rows = own.shape[0]
    query_blocks = rows // BLOCK
    group = max(g for g in range(1, GROUP + 1) if query_blocks % g == 0)
    slots = lists.shape[1]
    kernel = functools.partial(
        attend_kernel, inverse_root=1.0 / math.sqrt(head_size), head_size=head_size
    )
    grid_spec = pltpu.PrefetchScalarGridSpec(
        num_scalar_prefetch=3,
        grid=(query_blocks // group,),
        in_specs=[
            pl.BlockSpec((group * BLOCK, head_size), lambda b, *_: (b, 0)),
            pl.BlockSpec(memory_space=pl.ANY),
            pl.BlockSpec(memory_space=pl.ANY),
        ],
        out_specs=pl.BlockSpec((group * BLOCK, head_size), lambda b, *_: (b, 0)),
        scratch_shapes=[
            pltpu.VMEM((2 * other.shape[0] + BLOCK, 2 * head_size), own.dtype),
            pltpu.VMEM((group, slots * BLOCK, head_size), own.dtype),
            pltpu.VMEM((group, slots * BLOCK, head_size), own.dtype),
            pltpu.SemaphoreType.DMA((2,)),
        ],
    )
    return pl.pallas_call(
        kernel,
        grid_spec=grid_spec,
        out_shape=jax.ShapeDtypeStruct((rows, head_size), jnp.bfloat16),
        compiler_params=pltpu.CompilerParams(dimension_semantics=("arbitrary",)),
    )(lists, counts, narrow, own, own, other)


def per_device(queries, keys, values, block_lists, block_counts):
    rows = queries.shape[0]
    width = lax.axis_size("wide")
    head_size = queries.shape[1] // width
    stacked = jnp.concatenate(
        [a.reshape(rows, width, head_size) for a in (queries, keys, values)], axis=2
    )
    own = lax.all_to_all(stacked, "wide", split_axis=1, concat_axis=0, tiled=True)
    own = own.reshape(rows * width, 3 * head_size)
    other = lax.ppermute(own[:, head_size:], "narrow", [(0, 1), (1, 0)])
    narrow = lax.axis_index("narrow").astype(jnp.int32).reshape(1)
    attended = attend(own, other, block_lists[0], block_counts[0], narrow, head_size)
    return lax.all_to_all(attended, "wide", split_axis=0, concat_axis=1, tiled=True)


def solution(mesh):
    in_specs = (
        P(("groups", "narrow", "wide"), None),
        P(("groups", "narrow", "wide"), None),
        P(("groups", "narrow", "wide"), None),
        P(("groups", "wide"), "narrow", None),
        P(("groups", "wide"), "narrow"),
    )
    out_specs = P(("groups", "narrow", "wide"), None)
    return jax.shard_map(
        per_device, mesh=mesh, in_specs=in_specs, out_specs=out_specs, check_vma=False
    )
```

```python
import functools
import math

import jax
import jax.numpy as jnp
from jax import lax
from jax.experimental import pallas as pl
from jax.experimental.pallas import tpu as pltpu
from jax.sharding import PartitionSpec as P

BLOCK = 128
GROUP = 16


def attend_kernel(
    lists_ref,
    counts_ref,
    narrow_ref,
    q_ref,
    own_ref,
    other_ref,
    o_ref,
    table,
    kbuf,
    vbuf,
    sems,
    *,
    inverse_root,
    head_size,
):
    step = pl.program_id(0)
    half_rows = other_ref.shape[0]
    n = narrow_ref[0]

    @pl.when(step == 0)
    def _():
        own_copy = pltpu.make_async_copy(
            own_ref.at[:, pl.ds(head_size, 2 * head_size)],
            table.at[pl.ds(n * half_rows, half_rows), :],
            sems.at[0],
        )
        other_copy = pltpu.make_async_copy(
            other_ref, table.at[pl.ds((1 - n) * half_rows, half_rows), :], sems.at[1]
        )
        own_copy.start()
        other_copy.start()
        own_copy.wait()
        other_copy.wait()

    group = q_ref.shape[0] // BLOCK
    slots = lists_ref.shape[1]
    key_blocks = 2 * half_rows // BLOCK
    zero_block = key_blocks

    @pl.when(step == 0)
    def _():
        table[pl.ds(zero_block * BLOCK, BLOCK), :] = jnp.zeros((BLOCK, table.shape[1]), table.dtype)

    for g in range(group):
        b = step * group + g
        count = counts_ref[b]
        first = lists_ref[b, 0]
        for j in range(slots):
            index = jnp.where(j < count, lists_ref[b, j], first)
            index = jnp.minimum(jnp.maximum(index, 0), key_blocks - 1)
            value_index = jnp.where(j < count, index, zero_block)
            start = pl.multiple_of(index * BLOCK, BLOCK)
            value_start = pl.multiple_of(value_index * BLOCK, BLOCK)
            kbuf[g, pl.ds(j * BLOCK, BLOCK), :] = table[pl.ds(start, BLOCK), pl.ds(0, head_size)]
            vbuf[g, pl.ds(j * BLOCK, BLOCK), :] = table[
                pl.ds(value_start, BLOCK), pl.ds(head_size, head_size)
            ]

    exponent_scale = inverse_root * math.log2(math.e)
    for g in range(group):
        rows = pl.ds(g * BLOCK, BLOCK)
        count = counts_ref[step * group + g]
        raw_scores = lax.dot_general(
            q_ref[rows, :],
            kbuf[g],
            (((1,), (1,)), ((), ())),
            preferred_element_type=jnp.float32,
        )
        raw_max = jnp.max(raw_scores, axis=1, keepdims=True)
        weights = jnp.exp2((raw_scores - raw_max) * exponent_scale)
        padded = (slots - count).astype(jnp.float32)
        row_total = jnp.sum(weights, axis=1, keepdims=True) - padded * jnp.sum(
            weights[:, :BLOCK], axis=1, keepdims=True
        )
        weighted_sum = jnp.dot(
            weights.astype(jnp.bfloat16), vbuf[g], preferred_element_type=jnp.float32
        )
        o_ref[rows, :] = (weighted_sum / row_total).astype(o_ref.dtype)


def attend(own, other, lists, counts, narrow, head_size):
    rows = own.shape[0]
    query_blocks = rows // BLOCK
    group = max(g for g in range(1, GROUP + 1) if query_blocks % g == 0)
    slots = lists.shape[1]
    kernel = functools.partial(
        attend_kernel, inverse_root=1.0 / math.sqrt(head_size), head_size=head_size
    )
    grid_spec = pltpu.PrefetchScalarGridSpec(
        num_scalar_prefetch=3,
        grid=(query_blocks // group,),
        in_specs=[
            pl.BlockSpec((group * BLOCK, head_size), lambda b, *_: (b, 0)),
            pl.BlockSpec(memory_space=pl.ANY),
            pl.BlockSpec(memory_space=pl.ANY),
        ],
        out_specs=pl.BlockSpec((group * BLOCK, head_size), lambda b, *_: (b, 0)),
        scratch_shapes=[
            pltpu.VMEM((2 * other.shape[0] + BLOCK, 2 * head_size), own.dtype),
            pltpu.VMEM((group, slots * BLOCK, head_size), own.dtype),
            pltpu.VMEM((group, slots * BLOCK, head_size), own.dtype),
            pltpu.SemaphoreType.DMA((2,)),
        ],
    )
    return pl.pallas_call(
        kernel,
        grid_spec=grid_spec,
        out_shape=jax.ShapeDtypeStruct((rows, head_size), jnp.bfloat16),
        compiler_params=pltpu.CompilerParams(dimension_semantics=("arbitrary",)),
    )(lists, counts, narrow, own, own, other)


def per_device(queries, keys, values, block_lists, block_counts):
    rows = queries.shape[0]
    width = lax.axis_size("wide")
    head_size = queries.shape[1] // width
    stacked = jnp.concatenate(
        [a.reshape(rows, width, head_size) for a in (queries, keys, values)], axis=2
    )
    own = lax.all_to_all(stacked, "wide", split_axis=1, concat_axis=0, tiled=True)
    own = own.reshape(rows * width, 3 * head_size)
    other = lax.ppermute(own[:, head_size:], "narrow", [(0, 1), (1, 0)])
    narrow = lax.axis_index("narrow").astype(jnp.int32).reshape(1)
    attended = attend(own, other, block_lists[0], block_counts[0], narrow, head_size)
    return lax.all_to_all(attended, "wide", split_axis=0, concat_axis=1, tiled=True)


def solution(mesh):
    in_specs = (
        P(("groups", "narrow", "wide"), None),
        P(("groups", "narrow", "wide"), None),
        P(("groups", "narrow", "wide"), None),
        P(("groups", "wide"), "narrow", None),
        P(("groups", "wide"), "narrow"),
    )
    out_specs = P(("groups", "narrow", "wide"), None)
    return jax.shard_map(
        per_device, mesh=mesh, in_specs=in_specs, out_specs=out_specs, check_vma=False
    )
```

```python
import functools
import math

import jax
import jax.numpy as jnp
from jax import lax
from jax.experimental import pallas as pl
from jax.experimental.pallas import tpu as pltpu
from jax.sharding import PartitionSpec as P

BLOCK = 128
GROUP = 8


def attend_kernel(
    lists_ref,
    counts_ref,
    narrow_ref,
    q_ref,
    own_ref,
    other_ref,
    o_ref,
    table,
    sems,
    *,
    inverse_root,
    head_size,
):
    step = pl.program_id(0)
    half_rows = other_ref.shape[0]
    n = narrow_ref[0]

    @pl.when(step == 0)
    def _():
        own_copy = pltpu.make_async_copy(
            own_ref.at[:, pl.ds(head_size, 2 * head_size)],
            table.at[pl.ds(n * half_rows, half_rows), :],
            sems.at[0],
        )
        other_copy = pltpu.make_async_copy(
            other_ref, table.at[pl.ds((1 - n) * half_rows, half_rows), :], sems.at[1]
        )
        own_copy.start()
        other_copy.start()
        own_copy.wait()
        other_copy.wait()

    group = q_ref.shape[0] // BLOCK
    slots = lists_ref.shape[1]
    key_blocks = 2 * half_rows // BLOCK
    zero_block = key_blocks

    @pl.when(step == 0)
    def _():
        table[pl.ds(zero_block * BLOCK, BLOCK), :] = jnp.zeros((BLOCK, table.shape[1]), table.dtype)

    exponent_scale = inverse_root * math.log2(math.e)
    for g in range(group):
        rows = pl.ds(g * BLOCK, BLOCK)
        b = step * group + g
        count = counts_ref[b]
        first = lists_ref[b, 0]
        queries = q_ref[rows, :]
        value_starts, parts = [], []
        for j in range(slots):
            index = jnp.where(j < count, lists_ref[b, j], first)
            index = jnp.minimum(jnp.maximum(index, 0), key_blocks - 1)
            value_index = jnp.where(j < count, index, zero_block)
            start = pl.multiple_of(index * BLOCK, BLOCK)
            value_starts.append(pl.multiple_of(value_index * BLOCK, BLOCK))
            parts.append(
                lax.dot_general(
                    queries,
                    table[pl.ds(start, BLOCK), pl.ds(0, head_size)],
                    (((1,), (1,)), ((), ())),
                    preferred_element_type=jnp.float32,
                )
            )
        raw_scores = jnp.concatenate(parts, axis=1)
        raw_max = jnp.max(raw_scores, axis=1, keepdims=True)
        weights = jnp.exp2((raw_scores - raw_max) * exponent_scale)
        padded = (slots - count).astype(jnp.float32)
        row_total = jnp.sum(weights, axis=1, keepdims=True) - padded * jnp.sum(
            weights[:, :BLOCK], axis=1, keepdims=True
        )
        rounded = weights.astype(jnp.bfloat16)
        weighted_sum = jnp.zeros((BLOCK, head_size), jnp.float32)
        for j in range(slots):
            weighted_sum = weighted_sum + jnp.dot(
                rounded[:, j * BLOCK : (j + 1) * BLOCK],
                table[pl.ds(value_starts[j], BLOCK), pl.ds(head_size, head_size)],
                preferred_element_type=jnp.float32,
            )
        o_ref[rows, :] = (weighted_sum / row_total).astype(o_ref.dtype)


def attend(own, other, lists, counts, narrow, head_size):
    rows = own.shape[0]
    query_blocks = rows // BLOCK
    group = max(g for g in range(1, GROUP + 1) if query_blocks % g == 0)
    slots = lists.shape[1]
    kernel = functools.partial(
        attend_kernel, inverse_root=1.0 / math.sqrt(head_size), head_size=head_size
    )
    grid_spec = pltpu.PrefetchScalarGridSpec(
        num_scalar_prefetch=3,
        grid=(query_blocks // group,),
        in_specs=[
            pl.BlockSpec((group * BLOCK, head_size), lambda b, *_: (b, 0)),
            pl.BlockSpec(memory_space=pl.ANY),
            pl.BlockSpec(memory_space=pl.ANY),
        ],
        out_specs=pl.BlockSpec((group * BLOCK, head_size), lambda b, *_: (b, 0)),
        scratch_shapes=[
            pltpu.VMEM((2 * other.shape[0] + BLOCK, 2 * head_size), own.dtype),
            pltpu.SemaphoreType.DMA((2,)),
        ],
    )
    return pl.pallas_call(
        kernel,
        grid_spec=grid_spec,
        out_shape=jax.ShapeDtypeStruct((rows, head_size), jnp.bfloat16),
        compiler_params=pltpu.CompilerParams(dimension_semantics=("arbitrary",)),
    )(lists, counts, narrow, own, own, other)


def per_device(queries, keys, values, block_lists, block_counts):
    rows = queries.shape[0]
    width = lax.axis_size("wide")
    head_size = queries.shape[1] // width
    stacked = jnp.concatenate(
        [a.reshape(rows, width, head_size) for a in (queries, keys, values)], axis=2
    )
    own = lax.all_to_all(stacked, "wide", split_axis=1, concat_axis=0, tiled=True)
    own = own.reshape(rows * width, 3 * head_size)
    other = lax.ppermute(own[:, head_size:], "narrow", [(0, 1), (1, 0)])
    narrow = lax.axis_index("narrow").astype(jnp.int32).reshape(1)
    attended = attend(own, other, block_lists[0], block_counts[0], narrow, head_size)
    return lax.all_to_all(attended, "wide", split_axis=0, concat_axis=1, tiled=True)


def solution(mesh):
    in_specs = (
        P(("groups", "narrow", "wide"), None),
        P(("groups", "narrow", "wide"), None),
        P(("groups", "narrow", "wide"), None),
        P(("groups", "wide"), "narrow", None),
        P(("groups", "wide"), "narrow"),
    )
    out_specs = P(("groups", "narrow", "wide"), None)
    return jax.shard_map(
        per_device, mesh=mesh, in_specs=in_specs, out_specs=out_specs, check_vma=False
    )
```

```python
import functools
import math

import jax
import jax.numpy as jnp
from jax import lax
from jax.experimental import pallas as pl
from jax.experimental.pallas import tpu as pltpu
from jax.sharding import PartitionSpec as P

BLOCK = 128
GROUP = 8


def attend_kernel(
    lists_ref,
    counts_ref,
    narrow_ref,
    q_ref,
    own_ref,
    other_lo_ref,
    other_hi_ref,
    o_ref,
    table,
    kbuf,
    vbuf,
    sems,
    *,
    inverse_root,
    head_size,
):
    step = pl.program_id(0)
    half_rows = 2 * other_lo_ref.shape[0]
    piece = other_lo_ref.shape[0]
    n = narrow_ref[0]

    @pl.when(step == 0)
    def _():
        own_copy = pltpu.make_async_copy(
            own_ref.at[:, pl.ds(head_size, 2 * head_size)],
            table.at[pl.ds(n * half_rows, half_rows), :],
            sems.at[0],
        )
        lo_copy = pltpu.make_async_copy(
            other_lo_ref, table.at[pl.ds((1 - n) * half_rows, piece), :], sems.at[1]
        )
        hi_copy = pltpu.make_async_copy(
            other_hi_ref, table.at[pl.ds((1 - n) * half_rows + piece, piece), :], sems.at[2]
        )
        own_copy.start()
        lo_copy.start()
        hi_copy.start()
        own_copy.wait()
        lo_copy.wait()
        hi_copy.wait()

    group = q_ref.shape[0] // BLOCK
    slots = lists_ref.shape[1]
    key_blocks = 2 * half_rows // BLOCK
    zero_block = key_blocks

    @pl.when(step == 0)
    def _():
        table[pl.ds(zero_block * BLOCK, BLOCK), :] = jnp.zeros((BLOCK, table.shape[1]), table.dtype)

    for g in range(group):
        b = step * group + g
        count = counts_ref[b]
        first = lists_ref[b, 0]
        for j in range(slots):
            index = jnp.where(j < count, lists_ref[b, j], first)
            index = jnp.minimum(jnp.maximum(index, 0), key_blocks - 1)
            value_index = jnp.where(j < count, index, zero_block)
            start = pl.multiple_of(index * BLOCK, BLOCK)
            value_start = pl.multiple_of(value_index * BLOCK, BLOCK)
            kbuf[g, pl.ds(j * BLOCK, BLOCK), :] = table[pl.ds(start, BLOCK), pl.ds(0, head_size)]
            vbuf[g, pl.ds(j * BLOCK, BLOCK), :] = table[
                pl.ds(value_start, BLOCK), pl.ds(head_size, head_size)
            ]

    exponent_scale = inverse_root * math.log2(math.e)
    for g in range(group):
        rows = pl.ds(g * BLOCK, BLOCK)
        count = counts_ref[step * group + g]
        raw_scores = lax.dot_general(
            q_ref[rows, :],
            kbuf[g],
            (((1,), (1,)), ((), ())),
            preferred_element_type=jnp.float32,
        )
        raw_max = jnp.max(raw_scores, axis=1, keepdims=True)
        weights = jnp.exp2((raw_scores - raw_max) * exponent_scale)
        padded = (slots - count).astype(jnp.float32)
        row_total = jnp.sum(weights, axis=1, keepdims=True) - padded * jnp.sum(
            weights[:, :BLOCK], axis=1, keepdims=True
        )
        weighted_sum = jnp.dot(
            weights.astype(jnp.bfloat16), vbuf[g], preferred_element_type=jnp.float32
        )
        o_ref[rows, :] = (weighted_sum / row_total).astype(o_ref.dtype)


def attend(own, other_lo, other_hi, lists, counts, narrow, head_size):
    rows = own.shape[0]
    query_blocks = rows // BLOCK
    group = max(g for g in range(1, GROUP + 1) if query_blocks % g == 0)
    slots = lists.shape[1]
    kernel = functools.partial(
        attend_kernel, inverse_root=1.0 / math.sqrt(head_size), head_size=head_size
    )
    grid_spec = pltpu.PrefetchScalarGridSpec(
        num_scalar_prefetch=3,
        grid=(query_blocks // group,),
        in_specs=[
            pl.BlockSpec((group * BLOCK, head_size), lambda b, *_: (b, 0)),
            pl.BlockSpec(memory_space=pl.ANY),
            pl.BlockSpec(memory_space=pl.ANY),
            pl.BlockSpec(memory_space=pl.ANY),
        ],
        out_specs=pl.BlockSpec((group * BLOCK, head_size), lambda b, *_: (b, 0)),
        scratch_shapes=[
            pltpu.VMEM((own.shape[0] * 2 + BLOCK, 2 * head_size), own.dtype),
            pltpu.VMEM((group, slots * BLOCK, head_size), own.dtype),
            pltpu.VMEM((group, slots * BLOCK, head_size), own.dtype),
            pltpu.SemaphoreType.DMA((3,)),
        ],
    )
    return pl.pallas_call(
        kernel,
        grid_spec=grid_spec,
        out_shape=jax.ShapeDtypeStruct((rows, head_size), jnp.bfloat16),
        compiler_params=pltpu.CompilerParams(dimension_semantics=("arbitrary",)),
    )(lists, counts, narrow, own, own, other_lo, other_hi)


def per_device(queries, keys, values, block_lists, block_counts):
    rows = queries.shape[0]
    width = lax.axis_size("wide")
    head_size = queries.shape[1] // width
    stacked = jnp.concatenate(
        [a.reshape(rows, width, head_size) for a in (queries, keys, values)], axis=2
    )
    own = lax.all_to_all(stacked, "wide", split_axis=1, concat_axis=0, tiled=True)
    own = own.reshape(rows * width, 3 * head_size)
    piece = own.shape[0] // 2
    other_lo, other_hi = (
        lax.ppermute(own[rows_, head_size:], "narrow", [(0, 1), (1, 0)])
        for rows_ in (slice(0, piece), slice(piece, None))
    )
    narrow = lax.axis_index("narrow").astype(jnp.int32).reshape(1)
    attended = attend(own, other_lo, other_hi, block_lists[0], block_counts[0], narrow, head_size)
    return lax.all_to_all(attended, "wide", split_axis=0, concat_axis=1, tiled=True)


def solution(mesh):
    in_specs = (
        P(("groups", "narrow", "wide"), None),
        P(("groups", "narrow", "wide"), None),
        P(("groups", "narrow", "wide"), None),
        P(("groups", "wide"), "narrow", None),
        P(("groups", "wide"), "narrow"),
    )
    out_specs = P(("groups", "narrow", "wide"), None)
    return jax.shard_map(
        per_device, mesh=mesh, in_specs=in_specs, out_specs=out_specs, check_vma=False
    )
```

```python
import functools
import math

import jax
import jax.numpy as jnp
from jax import lax
from jax.experimental import pallas as pl
from jax.experimental.pallas import tpu as pltpu
from jax.sharding import PartitionSpec as P

BLOCK = 128
GROUP = 8


def attend_kernel(
    lists_ref,
    counts_ref,
    narrow_ref,
    q_ref,
    own_ref,
    other_ref,
    o_ref,
    table,
    kbuf,
    vbuf,
    sems,
    *,
    inverse_root,
    head_size,
):
    step = pl.program_id(0)
    half_rows = other_ref.shape[0]
    n = narrow_ref[0]

    group = q_ref.shape[0] // BLOCK
    slots = lists_ref.shape[1]
    key_blocks = 2 * half_rows // BLOCK
    zero_block = key_blocks

    @pl.when(step == 0)
    def _():
        table[pl.ds(zero_block * BLOCK, BLOCK), :] = jnp.zeros((BLOCK, table.shape[1]), table.dtype)

    def table_copies(part):
        own_copy = pltpu.make_async_copy(
            own_ref.at[:, pl.ds((1 + part) * head_size, head_size)],
            table.at[pl.ds(n * half_rows, half_rows), pl.ds(part * head_size, head_size)],
            sems.at[2 * part],
        )
        other_copy = pltpu.make_async_copy(
            other_ref.at[:, pl.ds(part * head_size, head_size)],
            table.at[pl.ds((1 - n) * half_rows, half_rows), pl.ds(part * head_size, head_size)],
            sems.at[2 * part + 1],
        )
        return own_copy, other_copy

    @pl.when(step == 0)
    def _():
        for copy in table_copies(0) + table_copies(1):
            copy.start()
        for copy in table_copies(0):
            copy.wait()

    starts = []
    for g in range(group):
        b = step * group + g
        count = counts_ref[b]
        first = lists_ref[b, 0]
        for j in range(slots):
            index = jnp.where(j < count, lists_ref[b, j], first)
            index = jnp.minimum(jnp.maximum(index, 0), key_blocks - 1)
            value_index = jnp.where(j < count, index, zero_block)
            start = pl.multiple_of(index * BLOCK, BLOCK)
            starts.append(pl.multiple_of(value_index * BLOCK, BLOCK))
            kbuf[g, pl.ds(j * BLOCK, BLOCK), :] = table[pl.ds(start, BLOCK), pl.ds(0, head_size)]

    @pl.when(step == 0)
    def _():
        for copy in table_copies(1):
            copy.wait()

    for g in range(group):
        for j in range(slots):
            vbuf[g, pl.ds(j * BLOCK, BLOCK), :] = table[
                pl.ds(starts[g * slots + j], BLOCK), pl.ds(head_size, head_size)
            ]

    exponent_scale = inverse_root * math.log2(math.e)
    for g in range(group):
        rows = pl.ds(g * BLOCK, BLOCK)
        count = counts_ref[step * group + g]
        raw_scores = lax.dot_general(
            q_ref[rows, :],
            kbuf[g],
            (((1,), (1,)), ((), ())),
            preferred_element_type=jnp.float32,
        )
        raw_max = jnp.max(raw_scores, axis=1, keepdims=True)
        weights = jnp.exp2((raw_scores - raw_max) * exponent_scale)
        padded = (slots - count).astype(jnp.float32)
        row_total = jnp.sum(weights, axis=1, keepdims=True) - padded * jnp.sum(
            weights[:, :BLOCK], axis=1, keepdims=True
        )
        weighted_sum = jnp.dot(
            weights.astype(jnp.bfloat16), vbuf[g], preferred_element_type=jnp.float32
        )
        o_ref[rows, :] = (weighted_sum / row_total).astype(o_ref.dtype)


def attend(own, other, lists, counts, narrow, head_size):
    rows = own.shape[0]
    query_blocks = rows // BLOCK
    group = max(g for g in range(1, GROUP + 1) if query_blocks % g == 0)
    slots = lists.shape[1]
    kernel = functools.partial(
        attend_kernel, inverse_root=1.0 / math.sqrt(head_size), head_size=head_size
    )
    grid_spec = pltpu.PrefetchScalarGridSpec(
        num_scalar_prefetch=3,
        grid=(query_blocks // group,),
        in_specs=[
            pl.BlockSpec((group * BLOCK, head_size), lambda b, *_: (b, 0)),
            pl.BlockSpec(memory_space=pl.ANY),
            pl.BlockSpec(memory_space=pl.ANY),
        ],
        out_specs=pl.BlockSpec((group * BLOCK, head_size), lambda b, *_: (b, 0)),
        scratch_shapes=[
            pltpu.VMEM((2 * other.shape[0] + BLOCK, 2 * head_size), own.dtype),
            pltpu.VMEM((group, slots * BLOCK, head_size), own.dtype),
            pltpu.VMEM((group, slots * BLOCK, head_size), own.dtype),
            pltpu.SemaphoreType.DMA((4,)),
        ],
    )
    return pl.pallas_call(
        kernel,
        grid_spec=grid_spec,
        out_shape=jax.ShapeDtypeStruct((rows, head_size), jnp.bfloat16),
        compiler_params=pltpu.CompilerParams(dimension_semantics=("arbitrary",)),
    )(lists, counts, narrow, own, own, other)


def per_device(queries, keys, values, block_lists, block_counts):
    rows = queries.shape[0]
    width = lax.axis_size("wide")
    head_size = queries.shape[1] // width
    stacked = (
        jnp.concatenate([queries, keys, values], axis=1)
        .reshape(rows, 3, width, head_size)
        .transpose(0, 2, 1, 3)
        .reshape(rows, width, 3 * head_size)
    )
    own = lax.all_to_all(stacked, "wide", split_axis=1, concat_axis=0, tiled=True)
    own = own.reshape(rows * width, 3 * head_size)
    other = lax.ppermute(own[:, head_size:], "narrow", [(0, 1), (1, 0)])
    narrow = lax.axis_index("narrow").astype(jnp.int32).reshape(1)
    attended = attend(own, other, block_lists[0], block_counts[0], narrow, head_size)
    return lax.all_to_all(attended, "wide", split_axis=0, concat_axis=1, tiled=True)


def solution(mesh):
    in_specs = (
        P(("groups", "narrow", "wide"), None),
        P(("groups", "narrow", "wide"), None),
        P(("groups", "narrow", "wide"), None),
        P(("groups", "wide"), "narrow", None),
        P(("groups", "wide"), "narrow"),
    )
    out_specs = P(("groups", "narrow", "wide"), None)
    return jax.shard_map(
        per_device, mesh=mesh, in_specs=in_specs, out_specs=out_specs, check_vma=False
    )
```

```python
import functools
import math

import jax
import jax.numpy as jnp
from jax import lax
from jax.experimental import pallas as pl
from jax.experimental.pallas import tpu as pltpu
from jax.sharding import PartitionSpec as P

BLOCK = 128
GROUP = 8


def attend_kernel(
    lists_ref,
    counts_ref,
    narrow_ref,
    q_ref,
    own_ref,
    other_ref,
    o_ref,
    table,
    kbuf,
    vbuf,
    sems,
    *,
    inverse_root,
    head_size,
):
    step = pl.program_id(0)
    half_rows = other_ref.shape[0]
    n = narrow_ref[0]

    @pl.when(step == 0)
    def _():
        own_copy = pltpu.make_async_copy(
            own_ref.at[:, pl.ds(head_size, 2 * head_size)],
            table.at[pl.ds(n * half_rows, half_rows), :],
            sems.at[0],
        )
        other_copy = pltpu.make_async_copy(
            other_ref, table.at[pl.ds((1 - n) * half_rows, half_rows), :], sems.at[1]
        )
        own_copy.start()
        other_copy.start()
        own_copy.wait()
        other_copy.wait()

    group = q_ref.shape[0] // BLOCK
    slots = lists_ref.shape[1]
    key_blocks = 2 * half_rows // BLOCK
    zero_block = key_blocks

    @pl.when(step == 0)
    def _():
        table[pl.ds(zero_block * BLOCK, BLOCK), :] = jnp.zeros((BLOCK, table.shape[1]), table.dtype)

    for g in range(group):
        b = step * group + g
        count = counts_ref[b]
        first = lists_ref[b, 0]
        for j in range(slots):
            index = jnp.where(j < count, lists_ref[b, j], first)
            index = jnp.minimum(jnp.maximum(index, 0), key_blocks - 1)
            value_index = jnp.where(j < count, index, zero_block)
            start = pl.multiple_of(index * BLOCK, BLOCK)
            value_start = pl.multiple_of(value_index * BLOCK, BLOCK)
            kbuf[g, pl.ds(j * BLOCK, BLOCK), :] = table[pl.ds(start, BLOCK), pl.ds(0, head_size)]
            vbuf[g, pl.ds(j * BLOCK, BLOCK), :] = table[
                pl.ds(value_start, BLOCK), pl.ds(head_size, head_size)
            ]

    exponent_scale = inverse_root * math.log2(math.e)
    for g in range(group):
        rows = pl.ds(g * BLOCK, BLOCK)
        count = counts_ref[step * group + g]
        raw_scores = lax.dot_general(
            q_ref[rows, :],
            kbuf[g],
            (((1,), (1,)), ((), ())),
            preferred_element_type=jnp.float32,
        )
        raw_max = jnp.max(raw_scores, axis=1, keepdims=True)
        weights = jnp.exp2((raw_scores - raw_max) * exponent_scale)
        padded = (slots - count).astype(jnp.float32)
        row_total = jnp.sum(weights, axis=1, keepdims=True) - padded * jnp.sum(
            weights[:, :BLOCK], axis=1, keepdims=True
        )
        weighted_sum = jnp.dot(
            weights.astype(jnp.bfloat16), vbuf[g], preferred_element_type=jnp.float32
        )
        o_ref[rows, :] = (weighted_sum / row_total).astype(o_ref.dtype)


def attend(own, other, lists, counts, narrow, head_size):
    rows = own.shape[0]
    query_blocks = rows // BLOCK
    group = max(g for g in range(1, GROUP + 1) if query_blocks % g == 0)
    slots = lists.shape[1]
    kernel = functools.partial(
        attend_kernel, inverse_root=1.0 / math.sqrt(head_size), head_size=head_size
    )
    grid_spec = pltpu.PrefetchScalarGridSpec(
        num_scalar_prefetch=3,
        grid=(query_blocks // group,),
        in_specs=[
            pl.BlockSpec((group * BLOCK, head_size), lambda b, *_: (b, 0)),
            pl.BlockSpec(memory_space=pl.ANY),
            pl.BlockSpec(memory_space=pl.ANY),
        ],
        out_specs=pl.BlockSpec((group * BLOCK, head_size), lambda b, *_: (b, 0)),
        scratch_shapes=[
            pltpu.VMEM((2 * other.shape[0] + BLOCK, 2 * head_size), own.dtype),
            pltpu.VMEM((group, slots * BLOCK, head_size), own.dtype),
            pltpu.VMEM((group, slots * BLOCK, head_size), own.dtype),
            pltpu.SemaphoreType.DMA((2,)),
        ],
    )
    return pl.pallas_call(
        kernel,
        grid_spec=grid_spec,
        out_shape=jax.ShapeDtypeStruct((rows, head_size), jnp.bfloat16),
        compiler_params=pltpu.CompilerParams(dimension_semantics=("arbitrary",)),
    )(lists, counts, narrow, own, own, other)


def per_device(queries, keys, values, block_lists, block_counts):
    rows = queries.shape[0]
    width = lax.axis_size("wide")
    head_size = queries.shape[1] // width
    stacked = (
        jnp.concatenate([queries, keys, values], axis=1)
        .reshape(rows, 3, width, head_size)
        .transpose(0, 2, 1, 3)
        .reshape(rows, width, 3 * head_size)
    )
    own = lax.all_to_all(stacked, "wide", split_axis=1, concat_axis=0, tiled=True)
    own = own.reshape(rows * width, 3 * head_size)
    other = lax.ppermute(own[:, head_size:], "narrow", [(0, 1), (1, 0)])
    narrow = lax.axis_index("narrow").astype(jnp.int32).reshape(1)
    attended = attend(own, other, block_lists[0], block_counts[0], narrow, head_size)
    return lax.all_to_all(attended, "wide", split_axis=0, concat_axis=1, tiled=True)


def solution(mesh):
    in_specs = (
        P(("groups", "narrow", "wide"), None),
        P(("groups", "narrow", "wide"), None),
        P(("groups", "narrow", "wide"), None),
        P(("groups", "wide"), "narrow", None),
        P(("groups", "wide"), "narrow"),
    )
    out_specs = P(("groups", "narrow", "wide"), None)
    return jax.shard_map(
        per_device, mesh=mesh, in_specs=in_specs, out_specs=out_specs, check_vma=False
    )
```

```python
import functools
import math

import jax
import jax.numpy as jnp
from jax import lax
from jax.experimental import pallas as pl
from jax.experimental.pallas import tpu as pltpu
from jax.sharding import PartitionSpec as P

BLOCK = 128
GROUP = 16


def attend_kernel(
    lists_ref,
    counts_ref,
    narrow_ref,
    q_ref,
    own_ref,
    other_ref,
    o_ref,
    table,
    kbuf,
    vbuf,
    sems,
    *,
    inverse_root,
    head_size,
):
    step = pl.program_id(0)
    half_rows = other_ref.shape[0]
    n = narrow_ref[0]

    @pl.when(step == 0)
    def _():
        own_copy = pltpu.make_async_copy(
            own_ref.at[:, pl.ds(head_size, 2 * head_size)],
            table.at[pl.ds(n * half_rows, half_rows), :],
            sems.at[0],
        )
        other_copy = pltpu.make_async_copy(
            other_ref, table.at[pl.ds((1 - n) * half_rows, half_rows), :], sems.at[1]
        )
        own_copy.start()
        other_copy.start()
        own_copy.wait()
        other_copy.wait()

    group = q_ref.shape[0] // BLOCK
    slots = lists_ref.shape[1]
    key_blocks = 2 * half_rows // BLOCK
    zero_block = key_blocks

    @pl.when(step == 0)
    def _():
        table[pl.ds(zero_block * BLOCK, BLOCK), :] = jnp.zeros((BLOCK, table.shape[1]), table.dtype)

    for g in range(group):
        b = step * group + g
        count = counts_ref[b]
        first = lists_ref[b, 0]
        for j in range(slots):
            index = jnp.where(j < count, lists_ref[b, j], first)
            index = jnp.minimum(jnp.maximum(index, 0), key_blocks - 1)
            value_index = jnp.where(j < count, index, zero_block)
            start = pl.multiple_of(index * BLOCK, BLOCK)
            value_start = pl.multiple_of(value_index * BLOCK, BLOCK)
            kbuf[g, pl.ds(j * BLOCK, BLOCK), :] = table[pl.ds(start, BLOCK), pl.ds(0, head_size)]
            vbuf[g, pl.ds(j * BLOCK, BLOCK), :] = table[
                pl.ds(value_start, BLOCK), pl.ds(head_size, head_size)
            ]

    exponent_scale = inverse_root * math.log2(math.e)
    for g in range(group):
        rows = pl.ds(g * BLOCK, BLOCK)
        count = counts_ref[step * group + g]
        raw_scores = lax.dot_general(
            q_ref[rows, :],
            kbuf[g],
            (((1,), (1,)), ((), ())),
            preferred_element_type=jnp.float32,
        )
        raw_max = jnp.max(raw_scores, axis=1, keepdims=True)
        weights = jnp.exp2((raw_scores - raw_max) * exponent_scale)
        padded = (slots - count).astype(jnp.float32)
        row_total = jnp.sum(weights, axis=1, keepdims=True) - padded * jnp.sum(
            weights[:, :BLOCK], axis=1, keepdims=True
        )
        weighted_sum = jnp.dot(
            weights.astype(jnp.bfloat16), vbuf[g], preferred_element_type=jnp.float32
        )
        o_ref[rows, :] = (weighted_sum / row_total).astype(o_ref.dtype)


def attend(own, other, lists, counts, narrow, head_size):
    rows = own.shape[0]
    query_blocks = rows // BLOCK
    group = max(g for g in range(1, GROUP + 1) if query_blocks % g == 0)
    slots = lists.shape[1]
    kernel = functools.partial(
        attend_kernel, inverse_root=1.0 / math.sqrt(head_size), head_size=head_size
    )
    grid_spec = pltpu.PrefetchScalarGridSpec(
        num_scalar_prefetch=3,
        grid=(query_blocks // group,),
        in_specs=[
            pl.BlockSpec((group * BLOCK, head_size), lambda b, *_: (b, 0)),
            pl.BlockSpec(memory_space=pl.ANY),
            pl.BlockSpec(memory_space=pl.ANY),
        ],
        out_specs=pl.BlockSpec((group * BLOCK, head_size), lambda b, *_: (b, 0)),
        scratch_shapes=[
            pltpu.VMEM((2 * other.shape[0] + BLOCK, 2 * head_size), own.dtype),
            pltpu.VMEM((group, slots * BLOCK, head_size), own.dtype),
            pltpu.VMEM((group, slots * BLOCK, head_size), own.dtype),
            pltpu.SemaphoreType.DMA((2,)),
        ],
    )
    return pl.pallas_call(
        kernel,
        grid_spec=grid_spec,
        out_shape=jax.ShapeDtypeStruct((rows, head_size), jnp.bfloat16),
        compiler_params=pltpu.CompilerParams(dimension_semantics=("arbitrary",)),
    )(lists, counts, narrow, own, own, other)


def per_device(queries, keys, values, block_lists, block_counts):
    rows = queries.shape[0]
    width = lax.axis_size("wide")
    head_size = queries.shape[1] // width
    stacked = (
        jnp.concatenate([queries, keys, values], axis=1)
        .reshape(rows, 3, width, head_size)
        .transpose(0, 2, 1, 3)
        .reshape(rows, width, 3 * head_size)
    )
    own = lax.all_to_all(stacked, "wide", split_axis=1, concat_axis=0, tiled=True)
    own = own.reshape(rows * width, 3 * head_size)
    other = lax.ppermute(own[:, head_size:], "narrow", [(0, 1), (1, 0)])
    narrow = lax.axis_index("narrow").astype(jnp.int32).reshape(1)
    attended = attend(own, other, block_lists[0], block_counts[0], narrow, head_size)
    return lax.all_to_all(attended, "wide", split_axis=0, concat_axis=1, tiled=True)


def solution(mesh):
    in_specs = (
        P(("groups", "narrow", "wide"), None),
        P(("groups", "narrow", "wide"), None),
        P(("groups", "narrow", "wide"), None),
        P(("groups", "wide"), "narrow", None),
        P(("groups", "wide"), "narrow"),
    )
    out_specs = P(("groups", "narrow", "wide"), None)
    return jax.shard_map(
        per_device, mesh=mesh, in_specs=in_specs, out_specs=out_specs, check_vma=False
    )
```

```python
import functools
import math

import jax
import jax.numpy as jnp
from jax import lax
from jax.experimental import pallas as pl
from jax.experimental.pallas import tpu as pltpu
from jax.sharding import PartitionSpec as P

BLOCK = 128
GROUP = 16


def attend_kernel(
    lists_ref,
    counts_ref,
    narrow_ref,
    q_ref,
    own_ref,
    other_ref,
    o_ref,
    table,
    qbuf,
    kbuf,
    vbuf,
    sems,
    *,
    inverse_root,
    head_size,
):
    step = pl.program_id(0)
    half_rows = other_ref.shape[0]
    n = narrow_ref[0]
    query_rows = qbuf.shape[0]
    query_copy = pltpu.make_async_copy(
        q_ref.at[pl.ds(pl.multiple_of(step * query_rows, BLOCK), query_rows), pl.ds(0, head_size)],
        qbuf,
        sems.at[2],
    )
    query_copy.start()

    @pl.when(step == 0)
    def _():
        own_copy = pltpu.make_async_copy(
            own_ref.at[:, pl.ds(head_size, 2 * head_size)],
            table.at[pl.ds(n * half_rows, half_rows), :],
            sems.at[0],
        )
        other_copy = pltpu.make_async_copy(
            other_ref, table.at[pl.ds((1 - n) * half_rows, half_rows), :], sems.at[1]
        )
        own_copy.start()
        other_copy.start()
        own_copy.wait()
        other_copy.wait()

    query_copy.wait()

    group = qbuf.shape[0] // BLOCK
    slots = lists_ref.shape[1]
    key_blocks = 2 * half_rows // BLOCK
    zero_block = key_blocks

    @pl.when(step == 0)
    def _():
        table[pl.ds(zero_block * BLOCK, BLOCK), :] = jnp.zeros((BLOCK, table.shape[1]), table.dtype)

    for g in range(group):
        b = step * group + g
        count = counts_ref[b]
        first = lists_ref[b, 0]
        for j in range(slots):
            index = jnp.where(j < count, lists_ref[b, j], first)
            index = jnp.minimum(jnp.maximum(index, 0), key_blocks - 1)
            value_index = jnp.where(j < count, index, zero_block)
            start = pl.multiple_of(index * BLOCK, BLOCK)
            value_start = pl.multiple_of(value_index * BLOCK, BLOCK)
            kbuf[g, pl.ds(j * BLOCK, BLOCK), :] = table[pl.ds(start, BLOCK), pl.ds(0, head_size)]
            vbuf[g, pl.ds(j * BLOCK, BLOCK), :] = table[
                pl.ds(value_start, BLOCK), pl.ds(head_size, head_size)
            ]

    exponent_scale = inverse_root * math.log2(math.e)
    for g in range(group):
        rows = pl.ds(g * BLOCK, BLOCK)
        count = counts_ref[step * group + g]
        raw_scores = lax.dot_general(
            qbuf[rows, :],
            kbuf[g],
            (((1,), (1,)), ((), ())),
            preferred_element_type=jnp.float32,
        )
        raw_max = jnp.max(raw_scores, axis=1, keepdims=True)
        weights = jnp.exp2((raw_scores - raw_max) * exponent_scale)
        padded = (slots - count).astype(jnp.float32)
        row_total = jnp.sum(weights, axis=1, keepdims=True) - padded * jnp.sum(
            weights[:, :BLOCK], axis=1, keepdims=True
        )
        weighted_sum = jnp.dot(
            weights.astype(jnp.bfloat16), vbuf[g], preferred_element_type=jnp.float32
        )
        o_ref[rows, :] = (weighted_sum / row_total).astype(o_ref.dtype)


def attend(own, other, lists, counts, narrow, head_size):
    rows = own.shape[0]
    query_blocks = rows // BLOCK
    group = max(g for g in range(1, GROUP + 1) if query_blocks % g == 0)
    slots = lists.shape[1]
    kernel = functools.partial(
        attend_kernel, inverse_root=1.0 / math.sqrt(head_size), head_size=head_size
    )
    grid_spec = pltpu.PrefetchScalarGridSpec(
        num_scalar_prefetch=3,
        grid=(query_blocks // group,),
        in_specs=[
            pl.BlockSpec(memory_space=pl.ANY),
            pl.BlockSpec(memory_space=pl.ANY),
            pl.BlockSpec(memory_space=pl.ANY),
        ],
        out_specs=pl.BlockSpec((group * BLOCK, head_size), lambda b, *_: (b, 0)),
        scratch_shapes=[
            pltpu.VMEM((2 * other.shape[0] + BLOCK, 2 * head_size), own.dtype),
            pltpu.VMEM((group * BLOCK, head_size), own.dtype),
            pltpu.VMEM((group, slots * BLOCK, head_size), own.dtype),
            pltpu.VMEM((group, slots * BLOCK, head_size), own.dtype),
            pltpu.SemaphoreType.DMA((3,)),
        ],
    )
    return pl.pallas_call(
        kernel,
        grid_spec=grid_spec,
        out_shape=jax.ShapeDtypeStruct((rows, head_size), jnp.bfloat16),
        compiler_params=pltpu.CompilerParams(dimension_semantics=("arbitrary",)),
    )(lists, counts, narrow, own, own, other)


def per_device(queries, keys, values, block_lists, block_counts):
    rows = queries.shape[0]
    width = lax.axis_size("wide")
    head_size = queries.shape[1] // width
    stacked = (
        jnp.concatenate([queries, keys, values], axis=1)
        .reshape(rows, 3, width, head_size)
        .transpose(0, 2, 1, 3)
        .reshape(rows, width, 3 * head_size)
    )
    own = lax.all_to_all(stacked, "wide", split_axis=1, concat_axis=0, tiled=True)
    own = own.reshape(rows * width, 3 * head_size)
    other = lax.ppermute(own[:, head_size:], "narrow", [(0, 1), (1, 0)])
    narrow = lax.axis_index("narrow").astype(jnp.int32).reshape(1)
    attended = attend(own, other, block_lists[0], block_counts[0], narrow, head_size)
    return lax.all_to_all(attended, "wide", split_axis=0, concat_axis=1, tiled=True)


def solution(mesh):
    in_specs = (
        P(("groups", "narrow", "wide"), None),
        P(("groups", "narrow", "wide"), None),
        P(("groups", "narrow", "wide"), None),
        P(("groups", "wide"), "narrow", None),
        P(("groups", "wide"), "narrow"),
    )
    out_specs = P(("groups", "narrow", "wide"), None)
    return jax.shard_map(
        per_device, mesh=mesh, in_specs=in_specs, out_specs=out_specs, check_vma=False
    )
```

```python
import functools
import math

import jax
import jax.numpy as jnp
from jax import lax
from jax.experimental import pallas as pl
from jax.experimental.pallas import tpu as pltpu
from jax.sharding import PartitionSpec as P

BLOCK = 128
GROUP = 16


def attend_kernel(
    lists_ref,
    counts_ref,
    narrow_ref,
    q_ref,
    own_ref,
    other_ref,
    o_ref,
    table,
    qbuf,
    obuf,
    kbuf,
    vbuf,
    sems,
    *,
    inverse_root,
    head_size,
):
    step = pl.program_id(0)
    half_rows = other_ref.shape[0]
    n = narrow_ref[0]
    query_rows = qbuf.shape[0]
    query_copy = pltpu.make_async_copy(
        q_ref.at[pl.ds(pl.multiple_of(step * query_rows, BLOCK), query_rows), pl.ds(0, head_size)],
        qbuf,
        sems.at[2],
    )
    query_copy.start()

    @pl.when(step == 0)
    def _():
        own_copy = pltpu.make_async_copy(
            own_ref.at[:, pl.ds(head_size, 2 * head_size)],
            table.at[pl.ds(n * half_rows, half_rows), :],
            sems.at[0],
        )
        other_copy = pltpu.make_async_copy(
            other_ref, table.at[pl.ds((1 - n) * half_rows, half_rows), :], sems.at[1]
        )
        own_copy.start()
        other_copy.start()
        own_copy.wait()
        other_copy.wait()

    query_copy.wait()

    group = qbuf.shape[0] // BLOCK
    slots = lists_ref.shape[1]
    key_blocks = 2 * half_rows // BLOCK
    zero_block = key_blocks

    @pl.when(step == 0)
    def _():
        table[pl.ds(zero_block * BLOCK, BLOCK), :] = jnp.zeros((BLOCK, table.shape[1]), table.dtype)

    for g in range(group):
        b = step * group + g
        count = counts_ref[b]
        first = lists_ref[b, 0]
        for j in range(slots):
            index = jnp.where(j < count, lists_ref[b, j], first)
            index = jnp.minimum(jnp.maximum(index, 0), key_blocks - 1)
            value_index = jnp.where(j < count, index, zero_block)
            start = pl.multiple_of(index * BLOCK, BLOCK)
            value_start = pl.multiple_of(value_index * BLOCK, BLOCK)
            kbuf[g, pl.ds(j * BLOCK, BLOCK), :] = table[pl.ds(start, BLOCK), pl.ds(0, head_size)]
            vbuf[g, pl.ds(j * BLOCK, BLOCK), :] = table[
                pl.ds(value_start, BLOCK), pl.ds(head_size, head_size)
            ]

    exponent_scale = inverse_root * math.log2(math.e)
    out_copies = []
    for g in range(group):
        rows = pl.ds(g * BLOCK, BLOCK)
        count = counts_ref[step * group + g]
        raw_scores = lax.dot_general(
            qbuf[rows, :],
            kbuf[g],
            (((1,), (1,)), ((), ())),
            preferred_element_type=jnp.float32,
        )
        raw_max = jnp.max(raw_scores, axis=1, keepdims=True)
        weights = jnp.exp2((raw_scores - raw_max) * exponent_scale)
        padded = (slots - count).astype(jnp.float32)
        row_total = jnp.sum(weights, axis=1, keepdims=True) - padded * jnp.sum(
            weights[:, :BLOCK], axis=1, keepdims=True
        )
        weighted_sum = jnp.dot(
            weights.astype(jnp.bfloat16), vbuf[g], preferred_element_type=jnp.float32
        )
        obuf[rows, :] = (weighted_sum / row_total).astype(obuf.dtype)
        out_copy = pltpu.make_async_copy(
            obuf.at[rows, :],
            o_ref.at[pl.ds(pl.multiple_of(step * query_rows + g * BLOCK, BLOCK), BLOCK), :],
            sems.at[3 + g],
        )
        out_copy.start()
        out_copies.append(out_copy)
    for out_copy in out_copies:
        out_copy.wait()


def attend(own, other, lists, counts, narrow, head_size):
    rows = own.shape[0]
    query_blocks = rows // BLOCK
    group = max(g for g in range(1, GROUP + 1) if query_blocks % g == 0)
    slots = lists.shape[1]
    kernel = functools.partial(
        attend_kernel, inverse_root=1.0 / math.sqrt(head_size), head_size=head_size
    )
    grid_spec = pltpu.PrefetchScalarGridSpec(
        num_scalar_prefetch=3,
        grid=(query_blocks // group,),
        in_specs=[
            pl.BlockSpec(memory_space=pl.ANY),
            pl.BlockSpec(memory_space=pl.ANY),
            pl.BlockSpec(memory_space=pl.ANY),
        ],
        out_specs=pl.BlockSpec(memory_space=pl.ANY),
        scratch_shapes=[
            pltpu.VMEM((2 * other.shape[0] + BLOCK, 2 * head_size), own.dtype),
            pltpu.VMEM((group * BLOCK, head_size), own.dtype),
            pltpu.VMEM((group * BLOCK, head_size), jnp.bfloat16),
            pltpu.VMEM((group, slots * BLOCK, head_size), own.dtype),
            pltpu.VMEM((group, slots * BLOCK, head_size), own.dtype),
            pltpu.SemaphoreType.DMA((3 + group,)),
        ],
    )
    return pl.pallas_call(
        kernel,
        grid_spec=grid_spec,
        out_shape=jax.ShapeDtypeStruct((rows, head_size), jnp.bfloat16),
        compiler_params=pltpu.CompilerParams(dimension_semantics=("arbitrary",)),
    )(lists, counts, narrow, own, own, other)


def per_device(queries, keys, values, block_lists, block_counts):
    rows = queries.shape[0]
    width = lax.axis_size("wide")
    head_size = queries.shape[1] // width
    stacked = (
        jnp.concatenate([queries, keys, values], axis=1)
        .reshape(rows, 3, width, head_size)
        .transpose(0, 2, 1, 3)
        .reshape(rows, width, 3 * head_size)
    )
    own = lax.all_to_all(stacked, "wide", split_axis=1, concat_axis=0, tiled=True)
    own = own.reshape(rows * width, 3 * head_size)
    other = lax.ppermute(own[:, head_size:], "narrow", [(0, 1), (1, 0)])
    narrow = lax.axis_index("narrow").astype(jnp.int32).reshape(1)
    attended = attend(own, other, block_lists[0], block_counts[0], narrow, head_size)
    return lax.all_to_all(attended, "wide", split_axis=0, concat_axis=1, tiled=True)


def solution(mesh):
    in_specs = (
        P(("groups", "narrow", "wide"), None),
        P(("groups", "narrow", "wide"), None),
        P(("groups", "narrow", "wide"), None),
        P(("groups", "wide"), "narrow", None),
        P(("groups", "wide"), "narrow"),
    )
    out_specs = P(("groups", "narrow", "wide"), None)
    return jax.shard_map(
        per_device, mesh=mesh, in_specs=in_specs, out_specs=out_specs, check_vma=False
    )
```

```python
import functools
import math

import jax
import jax.numpy as jnp
from jax import lax
from jax.experimental import pallas as pl
from jax.experimental.pallas import tpu as pltpu
from jax.sharding import PartitionSpec as P

BLOCK = 128
GROUP = 16


def attend_kernel(
    lists_ref,
    counts_ref,
    narrow_ref,
    q_ref,
    own_ref,
    other_ref,
    o_ref,
    table,
    qbuf,
    kbuf,
    vbuf,
    sems,
    *,
    inverse_root,
    head_size,
):
    step = pl.program_id(0)
    half_rows = other_ref.shape[0]
    n = narrow_ref[0]
    query_rows = qbuf.shape[0]
    query_copy = pltpu.make_async_copy(
        q_ref.at[pl.ds(pl.multiple_of(step * query_rows, BLOCK), query_rows), pl.ds(0, head_size)],
        qbuf,
        sems.at[2],
    )
    query_copy.start()

    @pl.when(step == 0)
    def _():
        own_copy = pltpu.make_async_copy(
            own_ref.at[:, pl.ds(head_size, 2 * head_size)],
            table.at[pl.ds(n * half_rows, half_rows), :],
            sems.at[0],
        )
        other_copy = pltpu.make_async_copy(
            other_ref, table.at[pl.ds((1 - n) * half_rows, half_rows), :], sems.at[1]
        )
        own_copy.start()
        other_copy.start()
        own_copy.wait()
        other_copy.wait()

    query_copy.wait()

    group = qbuf.shape[0] // BLOCK
    slots = lists_ref.shape[1]
    key_blocks = 2 * half_rows // BLOCK
    zero_block = key_blocks

    @pl.when(step == 0)
    def _():
        table[pl.ds(zero_block * BLOCK, BLOCK), :] = jnp.zeros((BLOCK, table.shape[1]), table.dtype)

    for g in range(group):
        b = step * group + g
        count = counts_ref[b]
        first = lists_ref[b, 0]
        for j in range(slots):
            index = jnp.where(j < count, lists_ref[b, j], first)
            index = jnp.minimum(jnp.maximum(index, 0), key_blocks - 1)
            value_index = jnp.where(j < count, index, zero_block)
            start = pl.multiple_of(index * BLOCK, BLOCK)
            value_start = pl.multiple_of(value_index * BLOCK, BLOCK)
            kbuf[g, pl.ds(j * BLOCK, BLOCK), :] = table[pl.ds(start, BLOCK), pl.ds(0, head_size)]
            vbuf[g, pl.ds(j * BLOCK, BLOCK), :] = table[
                pl.ds(value_start, BLOCK), pl.ds(head_size, head_size)
            ]

    exponent_scale = inverse_root * math.log2(math.e)
    for g in range(group):
        rows = pl.ds(g * BLOCK, BLOCK)
        count = counts_ref[step * group + g]
        raw_scores = lax.dot_general(
            qbuf[rows, :],
            kbuf[g],
            (((1,), (1,)), ((), ())),
            preferred_element_type=jnp.float32,
        )
        raw_max = jnp.max(raw_scores, axis=1, keepdims=True)
        weights = jnp.exp2((raw_scores - raw_max) * exponent_scale)
        padded = (slots - count).astype(jnp.float32)
        slot_sums = weights[:, :BLOCK]
        for j in range(1, slots):
            slot_sums = slot_sums + weights[:, j * BLOCK : (j + 1) * BLOCK]
        row_total = jnp.sum(slot_sums - padded * weights[:, :BLOCK], axis=1, keepdims=True)
        weighted_sum = jnp.dot(
            weights.astype(jnp.bfloat16), vbuf[g], preferred_element_type=jnp.float32
        )
        o_ref[rows, :] = (weighted_sum / row_total).astype(o_ref.dtype)


def attend(own, other, lists, counts, narrow, head_size):
    rows = own.shape[0]
    query_blocks = rows // BLOCK
    group = max(g for g in range(1, GROUP + 1) if query_blocks % g == 0)
    slots = lists.shape[1]
    kernel = functools.partial(
        attend_kernel, inverse_root=1.0 / math.sqrt(head_size), head_size=head_size
    )
    grid_spec = pltpu.PrefetchScalarGridSpec(
        num_scalar_prefetch=3,
        grid=(query_blocks // group,),
        in_specs=[
            pl.BlockSpec(memory_space=pl.ANY),
            pl.BlockSpec(memory_space=pl.ANY),
            pl.BlockSpec(memory_space=pl.ANY),
        ],
        out_specs=pl.BlockSpec((group * BLOCK, head_size), lambda b, *_: (b, 0)),
        scratch_shapes=[
            pltpu.VMEM((2 * other.shape[0] + BLOCK, 2 * head_size), own.dtype),
            pltpu.VMEM((group * BLOCK, head_size), own.dtype),
            pltpu.VMEM((group, slots * BLOCK, head_size), own.dtype),
            pltpu.VMEM((group, slots * BLOCK, head_size), own.dtype),
            pltpu.SemaphoreType.DMA((3,)),
        ],
    )
    return pl.pallas_call(
        kernel,
        grid_spec=grid_spec,
        out_shape=jax.ShapeDtypeStruct((rows, head_size), jnp.bfloat16),
        compiler_params=pltpu.CompilerParams(dimension_semantics=("arbitrary",)),
    )(lists, counts, narrow, own, own, other)


def per_device(queries, keys, values, block_lists, block_counts):
    rows = queries.shape[0]
    width = lax.axis_size("wide")
    head_size = queries.shape[1] // width
    stacked = (
        jnp.concatenate([queries, keys, values], axis=1)
        .reshape(rows, 3, width, head_size)
        .transpose(0, 2, 1, 3)
        .reshape(rows, width, 3 * head_size)
    )
    own = lax.all_to_all(stacked, "wide", split_axis=1, concat_axis=0, tiled=True)
    own = own.reshape(rows * width, 3 * head_size)
    other = lax.ppermute(own[:, head_size:], "narrow", [(0, 1), (1, 0)])
    narrow = lax.axis_index("narrow").astype(jnp.int32).reshape(1)
    attended = attend(own, other, block_lists[0], block_counts[0], narrow, head_size)
    return lax.all_to_all(attended, "wide", split_axis=0, concat_axis=1, tiled=True)


def solution(mesh):
    in_specs = (
        P(("groups", "narrow", "wide"), None),
        P(("groups", "narrow", "wide"), None),
        P(("groups", "narrow", "wide"), None),
        P(("groups", "wide"), "narrow", None),
        P(("groups", "wide"), "narrow"),
    )
    out_specs = P(("groups", "narrow", "wide"), None)
    return jax.shard_map(
        per_device, mesh=mesh, in_specs=in_specs, out_specs=out_specs, check_vma=False
    )
```
